32 devices in a mesh: reel: 2 (over y), frame: 8 (over z, x), band: 1, chan: 2 (over core).
Axes of the slice: x: 2, y: 2, z: 4, core: 2. Of those that a mesh axis runs over, the one named last changes fastest.
Arguments:
- embed: bfloat16 [64, 256, 256], P(('reel', 'frame'), 'band', 'chan'), parts along dimension 0, may hold values from -6 to 6, as said below
- values: bfloat16 [64, 256, 256], P(('reel', 'frame'), 'band', 'chan'), parts along dimension 0, may hold values from -6 to 6
- match_frame: int32 [64, 2, 16], P(('reel', 'frame'), 'band'), parts along dimension 0, may hold values from -8 to 8, as said below
- match_block: int32 [64, 2, 16], P(('reel', 'frame'), 'band'), parts along dimension 0, may hold values from 0 to 1, as said below
- block_counts: int32 [64], P(('reel', 'frame')), parts along dimension 0, may hold values from 1 to 2, as said below
Outputs:
- denoised: bfloat16 [64, 256, 256], P(('reel', 'frame'), 'band', 'chan'), parts along dimension 0
The draws below stay inside these ranges and needn't reach their ends.
There are 2 independent parts, one for each index of `reel`. The reference program is written for one: setup_inputs(seed, part) draws one part's arguments, and reference() takes and returns one part's arrays. A program takes and returns all parts, laid end to end along the dimension named above; each array names one. Nothing has to cross between parts.
Inputs may be any that keep to these rules, and one draw needn't show every extreme that they name: `embed`: floats of order one. f + match_frame[f, q, k] is a frame of the segment; entries 0 and 1 of every list are the farthest backward and the farthest forward offsets within 8 that the segment allows. `match_block`: block q belongs to band q // 2; its list names blocks of that band or the block just before or just after the band. `block_counts`: some frame has all its blocks active.
All inputs are finite; a program needn't handle non-finite values.
Results may differ from the reference program's by a relative error of at most 0.0035.
Values may be sent and summed in bfloat16 or wider, within the bound.
No kernel may reach another device: no remote copies, remote signals or barrier semaphores. Data moves between devices by JAX's collectives and lax.ppermute only.
A program may use at most 64 MiB of HBM per device.

```python
import math
import jax
import jax.numpy as jnp
from jax import lax

W = 256
BLOCK = 128
K = 16
REACH = 8
NB = 2
NBLK = 2
NP = 256
NF = 32


def draw_embed(key, part):
    key_base = jax.random.fold_in(key, 12)
    base = jax.random.normal(key_base, (NF, NP, W), jnp.float32)
    return jnp.clip(base, -6.0, 6.0).astype(jnp.bfloat16)


def draw_match_frame(key, part):
    frame_ids = jnp.arange(NF, dtype=jnp.int32)[:, None, None]
    lowest = jnp.maximum(-REACH, -frame_ids)
    highest = jnp.minimum(REACH, NF - 1 - frame_ids)
    offsets = jax.random.randint(key, (NF, NBLK, K), lowest, highest + 1, dtype=jnp.int32)
    offsets = offsets.at[:, :, 0].set(jnp.broadcast_to(lowest[:, :, 0], (NF, NBLK)))
    offsets = offsets.at[:, :, 1].set(jnp.broadcast_to(highest[:, :, 0], (NF, NBLK)))
    return offsets.astype(jnp.int32)


def draw_match_block(key, part):
    block_ids = jnp.arange(NBLK, dtype=jnp.int32)[:, None]
    band_start = block_ids // NB * NB
    lowest = jnp.maximum(band_start - 1, 0)
    highest = jnp.minimum(band_start + NB, NBLK - 1)
    picks = jax.random.randint(key, (NF, NBLK, K), lowest, highest + 1, dtype=jnp.int32)
    return picks.astype(jnp.int32)


def draw_block_counts(key, part):
    key_counts = jax.random.fold_in(key, 21)
    key_full = jax.random.fold_in(key, 22)
    counts = jax.random.randint(key_counts, (NF,), 1, NBLK + 1, dtype=jnp.int32)
    chosen_frame = jax.random.randint(key_full, (), 0, NF, dtype=jnp.int32)
    counts = counts.at[chosen_frame].set(NBLK)
    return counts.astype(jnp.int32)


def level_of(own_key, shape, cuts, smallest, largest):
    def one(axis_at, parts):
        draws = jax.random.uniform(jax.random.fold_in(jax.random.fold_in(own_key, 6), axis_at), (parts,), jnp.float32, smallest / len(cuts), largest / len(cuts))
        return jnp.repeat(jnp.exp(draws), shape[axis_at] // parts).reshape((-1,) + (1,) * (len(shape) - axis_at - 1))

    gain = one(*cuts[0])
    for cut in cuts[1:]:
        gain = gain * one(*cut)
    return gain


def gaussian(rng, shape, deviation, bound, split=(), kind=jnp.bfloat16):
    array = deviation * jax.random.normal(rng, shape, jnp.float32)
    if split:
        array = array * level_of(rng, shape, split, -0.22, 0.18)
    return jnp.clip(array, -bound, bound).astype(kind)


def setup_inputs(seed: int = 0, part: int = 0) -> dict:
    arg_keys = jax.random.split(jax.random.key(seed), 6)
    own_keys = jax.random.split(jax.random.fold_in(arg_keys[5], part), 6)
    return {
        "embed": draw_embed(jax.random.fold_in(jax.random.fold_in(arg_keys[5], part), 71), part),
        "values": gaussian(own_keys[1], (NF, NP, W), 1.0, 6.0, ((0, 8), (2, 2))),
        "match_frame": draw_match_frame(jax.random.fold_in(jax.random.fold_in(arg_keys[5], part), 71), part),
        "match_block": draw_match_block(jax.random.fold_in(jax.random.fold_in(arg_keys[5], part), 71), part),
        "block_counts": draw_block_counts(jax.random.fold_in(jax.random.fold_in(arg_keys[5], part), 71), part),
    }


def reference(embed, values, match_frame, match_block, block_counts):
    frame_count = embed.shape[0]
    block_count = embed.shape[1] // BLOCK
    embed_blocks = embed.reshape(frame_count, block_count, BLOCK, W)
    value_blocks = values.reshape(frame_count, block_count, BLOCK, W)
    score_scale = 1.0 / math.sqrt(W)
    numerator = jnp.zeros((frame_count, block_count, BLOCK, W), jnp.float32)
    mass_sum = jnp.zeros((frame_count, block_count, BLOCK), jnp.float32)

    def visit(state_pair, frame):
        numer, masses = state_pair
        key_frames = (frame + match_frame[frame]).astype(jnp.int32)
        key_blocks = match_block[frame].astype(jnp.int32)
        queries = embed_blocks[frame].astype(jnp.float32)
        key_feat = embed_blocks[key_frames, key_blocks].astype(jnp.float32)
        key_vals = value_blocks[key_frames, key_blocks].astype(jnp.float32)
        score = jnp.einsum('bid,bkjd->bikj', queries, key_feat) * score_scale
        score = score.reshape(block_count, BLOCK, K * BLOCK)
        peak = lax.optimization_barrier(jnp.max(score, axis=-1, keepdims=True))
        exponent = jnp.exp(score - peak)
        prob = exponent / lax.optimization_barrier(jnp.sum(exponent, axis=-1, keepdims=True))
        attention = prob.astype(jnp.bfloat16)
        estimate = jnp.einsum('bin,bnc->bic', attention.astype(jnp.float32), key_vals.reshape(block_count, K * BLOCK, W)).astype(jnp.bfloat16)
        active = (jnp.arange(block_count, dtype=jnp.int32) < block_counts[frame]).astype(jnp.float32)
        masked = attention.astype(jnp.float32) * active[:, None, None]
        contrib = jnp.einsum('bin,bic->bnc', masked, estimate.astype(jnp.float32))
        contrib = contrib.reshape(block_count, K, BLOCK, W)
        weights_sum = lax.optimization_barrier(jnp.sum(prob * active[:, None, None], axis=1)).reshape(block_count, K, BLOCK)
        numer = numer.at[key_frames, key_blocks].add(contrib)
        masses = masses.at[key_frames, key_blocks].add(weights_sum)
        return ((numer, masses), None)
    (numerator, mass_sum), unused = lax.scan(visit, (numerator, mass_sum), jnp.arange(frame_count, dtype=jnp.int32))
    result = (numerator + value_blocks.astype(jnp.float32)) / (mass_sum[..., None] + 1.0)
    return result.reshape(frame_count, block_count * BLOCK, W).astype(jnp.bfloat16)
```

```python
import functools
import math

import jax
import jax.numpy as jnp
from jax import lax
from jax.experimental import pallas as pl
from jax.experimental.pallas import tpu as pltpu
from jax.sharding import PartitionSpec as P

W = 256
BLOCK = 128
K = 16
REACH = 8
MASS_ROWS = 16


def with_halo(x, sides, width):
    for axis, dim in sides:
        size, length = (lax.axis_size(axis), x.shape[dim])
        up = [(i, (i + 1) % size) for i in range(size - 1)]
        down = [(j, i) for i, j in up]
        last = lax.slice_in_dim(x, length - width, length, axis=dim)
        initial = lax.slice_in_dim(x, 0, width, axis=dim)
        before = lax.ppermute(last, axis, up)
        after = lax.ppermute(initial, axis, down)
        x = jnp.concatenate([before, x, after], axis=dim)
    return x


def passed_along(block, axis, distance):
    devices = range(lax.axis_size(axis))
    route = [(i - distance, i) for i in devices if i - distance in devices]
    return lax.ppermute(block, axis, route)


def aggregate_kernel(
    slot_ref, act_ref, *refs, slabs, per_slab, center, queries, half, blocks, rimmed, halo
):
    slab_refs = refs[:slabs]
    other_refs = refs[slabs : 2 * slabs]
    own_num_ref, own_mass_ref = refs[2 * slabs : 2 * slabs + 2]
    remote_refs = refs[2 * slabs + 2 : 3 * slabs + 1]
    key_a, key_v, key_b, acc, macc, score_ref, sems = refs[3 * slabs + 1 :]

    copies = []
    for s in range(slabs):
        dst = pl.ds(s * per_slab, per_slab)
        copies.append(
            pltpu.make_async_copy(slab_refs[s].at[:, :, pl.ds(0, half)], key_a.at[dst], sems.at[0, s])
        )
        copies.append(
            pltpu.make_async_copy(slab_refs[s].at[:, :, pl.ds(half, half)], key_v.at[dst], sems.at[1, s])
        )
        copies.append(pltpu.make_async_copy(other_refs[s], key_b.at[dst], sems.at[2, s]))
    for c in copies:
        c.start()
    acc[...] = jnp.zeros(acc.shape, acc.dtype)
    macc[...] = jnp.zeros(macc.shape, macc.dtype)
    for c in copies:
        c.wait()

    score_scale = 1.0 / math.sqrt(W)
    dims_t = (((1,), (1,)), ((), ()))

    def one_query(i, carry):
        q_slot = center + (i // blocks) * rimmed + halo + i % blocks
        qa = key_a[q_slot]
        qb = key_b[q_slot]
        slots = [slot_ref[i * K + k] for k in range(K)]
        for k in range(K):
            s = slots[k]
            part = lax.dot_general(qa, key_a[s], dims_t, preferred_element_type=jnp.float32)
            part = part + lax.dot_general(qb, key_b[s], dims_t, preferred_element_type=jnp.float32)
            score_ref[:, k * BLOCK : (k + 1) * BLOCK] = part * score_scale
        score = score_ref[...]
        peak = jnp.max(score, axis=-1, keepdims=True)
        exponent = jnp.exp(score - peak)
        prob = exponent / jnp.sum(exponent, axis=-1, keepdims=True)
        attention = prob.astype(jnp.bfloat16)
        estimate = jnp.zeros((BLOCK, half), jnp.float32)
        for k in range(K):
            estimate = estimate + jnp.dot(
                attention[:, k * BLOCK : (k + 1) * BLOCK],
                key_v[slots[k]],
                preferred_element_type=jnp.float32,
            )
        estimate = estimate.astype(jnp.bfloat16).astype(jnp.float32)
        active = act_ref[i].astype(jnp.float32)
        masked = (attention.astype(jnp.float32) * active).astype(jnp.bfloat16)
        estimate_t = estimate.T.astype(jnp.bfloat16)
        contrib_t = jnp.dot(estimate_t, masked, preferred_element_type=jnp.float32)
        weights = jnp.sum(prob * active, axis=0, keepdims=True)
        for k in range(K):
            s = slots[k]
            acc[s] = acc[s] + contrib_t[:, k * BLOCK : (k + 1) * BLOCK]
            macc[s] = macc[s] + weights[:, k * BLOCK : (k + 1) * BLOCK]
        return carry

    lax.fori_loop(0, queries, one_query, 0)

    own = pl.ds(center, per_slab)
    own_num_ref[...] = acc[own]
    own_mass_ref[...] = macc[own]
    remote = [s for s in range(slabs) if s * per_slab != center]
    for ref, s in zip(remote_refs, remote):
        rows = pl.ds(s * per_slab, per_slab)
        ref[:, :half, :] = acc[rows].astype(jnp.bfloat16)
        ref[:, half:, :] = jnp.broadcast_to(macc[rows], (per_slab, MASS_ROWS, BLOCK)).astype(
            jnp.bfloat16
        )


def shards(embed, values, match_frame, match_block, block_counts):
    frames = embed.shape[0]
    band_rows = embed.shape[1]
    half = embed.shape[2]
    blocks = band_rows // BLOCK
    hops = -(-REACH // frames)
    band_index = lax.axis_index("band")
    band_size = lax.axis_size("band")
    halo = 1 if band_size > 1 else 0
    chan_size = lax.axis_size("chan")
    chan_swap = [(i, (i + 1) % chan_size) for i in range(chan_size)]

    features = jnp.concatenate([embed, values], axis=2)
    if halo:
        features = with_halo(features, (("band", 1),), BLOCK)
    rimmed_blocks = blocks + 2 * halo
    per_slab = frames * rimmed_blocks
    window = []
    for offset in range(-hops, hops + 1):
        slab = features if offset == 0 else passed_along(features, "frame", -offset)
        window.append(slab.reshape(per_slab, BLOCK, 2 * half))
    others = [
        lax.ppermute(slab[:, :, :half], "chan", chan_swap) for slab in window
    ]
    slabs = len(window)
    center = hops * per_slab

    frame_ids = jnp.arange(frames, dtype=jnp.int32)
    key_rows = (hops * frames + frame_ids[:, None, None] + match_frame) * rimmed_blocks
    key_cols = match_block - band_index * blocks + halo
    slot = jnp.clip(key_rows + key_cols, 0, slabs * per_slab - 1).astype(jnp.int32).reshape(-1)
    block_ids = band_index * blocks + jnp.arange(blocks, dtype=jnp.int32)
    active = (block_ids[None, :] < block_counts[:, None]).astype(jnp.int32)
    queries = frames * blocks

    kernel = functools.partial(
        aggregate_kernel,
        slabs=slabs,
        per_slab=per_slab,
        center=center,
        queries=queries,
        half=half,
        blocks=blocks,
        rimmed=rimmed_blocks,
        halo=halo,
    )
    smem = pl.BlockSpec(memory_space=pltpu.SMEM)
    hbm = pl.BlockSpec(memory_space=pl.ANY)
    vmem = pl.BlockSpec(memory_space=pltpu.VMEM)
    out_shape = [
        jax.ShapeDtypeStruct((per_slab, half, BLOCK), jnp.float32),
        jax.ShapeDtypeStruct((per_slab, 1, BLOCK), jnp.float32),
    ] + [
        jax.ShapeDtypeStruct((per_slab, half + MASS_ROWS, BLOCK), jnp.bfloat16)
        for _ in range(slabs - 1)
    ]
    total = slabs * per_slab
    outs = pl.pallas_call(
        kernel,
        out_shape=out_shape,
        in_specs=[smem, smem] + [hbm] * (2 * slabs),
        out_specs=[vmem] * len(out_shape),
        scratch_shapes=[
            pltpu.VMEM((total, BLOCK, half), jnp.bfloat16),
            pltpu.VMEM((total, BLOCK, half), jnp.bfloat16),
            pltpu.VMEM((total, BLOCK, half), jnp.bfloat16),
            pltpu.VMEM((total, half, BLOCK), jnp.float32),
            pltpu.VMEM((total, 1, BLOCK), jnp.float32),
            pltpu.VMEM((BLOCK, K * BLOCK), jnp.float32),
            pltpu.SemaphoreType.DMA((3, slabs)),
        ],
    )(slot, active.reshape(-1), *window, *others)
    own_num, own_mass = outs[0], outs[1]
    remote = outs[2:]
    offsets = [o for o in range(-hops, hops + 1) if o != 0]
    for offset, outgoing in zip(offsets, remote):
        arrived = passed_along(outgoing, "frame", offset).astype(jnp.float32)
        own_num = own_num + arrived[:, :half, :]
        own_mass = own_mass + arrived[:, half : half + 1, :]
    own_num = own_num.reshape(frames, rimmed_blocks, half, BLOCK)
    own_mass = own_mass.reshape(frames, rimmed_blocks, BLOCK)
    if halo:
        for toward in (1, -1):
            rim_block = blocks + 1 if toward > 0 else 0
            target_block = 1 if toward > 0 else blocks
            arrived = (
                passed_along(own_num[:, rim_block].astype(jnp.bfloat16), "band", toward).astype(
                    jnp.float32
                ),
                passed_along(own_mass[:, rim_block].astype(jnp.bfloat16), "band", toward).astype(
                    jnp.float32
                ),
            )
            own_num = own_num.at[:, target_block].add(arrived[0])
            own_mass = own_mass.at[:, target_block].add(arrived[1])
        own_num = own_num[:, 1 : blocks + 1]
        own_mass = own_mass[:, 1 : blocks + 1]
    numer = jnp.swapaxes(own_num, -1, -2)
    value_blocks = values.reshape(frames, blocks, BLOCK, half).astype(jnp.float32)
    result = (numer + value_blocks) / (own_mass[..., None] + 1.0)
    return result.reshape(frames, band_rows, half).astype(jnp.bfloat16)


def solution(mesh):
    placed = (
        P(("reel", "frame"), "band", "chan"),
        P(("reel", "frame"), "band", "chan"),
        P(("reel", "frame"), "band", None),
        P(("reel", "frame"), "band", None),
        P(("reel", "frame")),
    )
    return jax.shard_map(
        shards,
        mesh=mesh,
        in_specs=placed,
        out_specs=P(("reel", "frame"), "band", "chan"),
        check_vma=False,
    )
```

```python
import functools
import math

import jax
import jax.numpy as jnp
from jax import lax
from jax.experimental import pallas as pl
from jax.experimental.pallas import tpu as pltpu
from jax.sharding import PartitionSpec as P

W = 256
BLOCK = 128
K = 16
REACH = 8
MASS_ROWS = 16


def with_halo(x, sides, width):
    for axis, dim in sides:
        size, length = (lax.axis_size(axis), x.shape[dim])
        up = [(i, (i + 1) % size) for i in range(size - 1)]
        down = [(j, i) for i, j in up]
        last = lax.slice_in_dim(x, length - width, length, axis=dim)
        initial = lax.slice_in_dim(x, 0, width, axis=dim)
        before = lax.ppermute(last, axis, up)
        after = lax.ppermute(initial, axis, down)
        x = jnp.concatenate([before, x, after], axis=dim)
    return x


def passed_along(block, axis, distance):
    devices = range(lax.axis_size(axis))
    route = [(i - distance, i) for i in devices if i - distance in devices]
    return lax.ppermute(block, axis, route)


def aggregate_kernel(
    slot_ref, act_ref, *refs, slabs, per_slab, center, queries, half, blocks, rimmed, halo
):
    slab_refs = refs[:slabs]
    other_refs = refs[slabs : 2 * slabs]
    own_num_ref, own_mass_ref = refs[2 * slabs : 2 * slabs + 2]
    remote_refs = refs[2 * slabs + 2 : 3 * slabs + 1]
    key_e, key_vt, acc, macc, key_stack, value_stack, sems, gather_sems = refs[3 * slabs + 1 :]

    copies = []
    for s in range(slabs):
        dst = pl.ds(s * per_slab, per_slab)
        mine = slab_refs[s].at[:, :, pl.ds(0, half)]
        copies.append(pltpu.make_async_copy(mine, key_e.at[dst, :, pl.ds(0, half)], sems.at[0, s]))
        theirs = key_e.at[dst, :, pl.ds(half, half)]
        copies.append(pltpu.make_async_copy(other_refs[s], theirs, sems.at[1, s]))
        vals = slab_refs[s].at[:, :, pl.ds(half, half)]
        copies.append(pltpu.make_async_copy(vals, key_vt.at[dst], sems.at[2, s]))
    for c in copies:
        c.start()
    acc[...] = jnp.zeros(acc.shape, acc.dtype)
    macc[...] = jnp.zeros(macc.shape, macc.dtype)
    for c in copies:
        c.wait()

    def gather(i, buf):
        out = []
        for k in range(K):
            s = slot_ref[i * K + k]
            rows = pl.ds(k * BLOCK, BLOCK)
            out.append(pltpu.make_async_copy(key_e.at[s], key_stack.at[buf, rows], gather_sems.at[buf, 0, k]))
            out.append(
                pltpu.make_async_copy(key_vt.at[s], value_stack.at[buf, :, rows], gather_sems.at[buf, 1, k])
            )
        return out

    for c in gather(0, 0):
        c.start()

    score_scale = 1.0 / math.sqrt(W)
    dims_t = (((1,), (1,)), ((), ()))

    def one_query(i, carry):
        buf = i % 2
        for c in gather(i, buf):
            c.wait()

        @pl.when(i + 1 < queries)
        def _():
            for c in gather(i + 1, 1 - buf):
                c.start()

        q_slot = center + (i // blocks) * rimmed + halo + i % blocks
        query = key_e[q_slot]
        score_t = lax.dot_general(key_stack[buf], query, dims_t, preferred_element_type=jnp.float32)
        score_t = score_t * score_scale
        peak = jnp.max(score_t, axis=0, keepdims=True)
        exponent = jnp.exp(score_t - peak)
        prob_t = exponent / jnp.sum(exponent, axis=0, keepdims=True)
        attention_t = prob_t.astype(jnp.bfloat16)
        estimate_t = jnp.dot(value_stack[buf], attention_t, preferred_element_type=jnp.float32)
        estimate_t = estimate_t.astype(jnp.bfloat16)
        active = act_ref[i].astype(jnp.float32)
        masked_t = attention_t * active.astype(jnp.bfloat16)
        contrib = lax.dot_general(masked_t, estimate_t, dims_t, preferred_element_type=jnp.float32)
        weights = jnp.sum(prob_t * active, axis=1, keepdims=True)
        for k in range(K):
            s = slot_ref[i * K + k]
            rows = slice(k * BLOCK, (k + 1) * BLOCK)
            acc[s] = acc[s] + contrib[rows]
            macc[s] = macc[s] + weights[rows]
        return carry

    lax.fori_loop(0, queries, one_query, 0)

    own = pl.ds(center, per_slab)
    own_num_ref[...] = acc[own]
    own_mass_ref[...] = macc[own]
    remote = [s for s in range(slabs) if s * per_slab != center]
    for ref, s in zip(remote_refs, remote):
        rows = pl.ds(s * per_slab, per_slab)
        ref[:, :BLOCK, :] = acc[rows].astype(jnp.bfloat16)
        for j in range(per_slab):
            spread = jnp.broadcast_to(macc[s * per_slab + j], (BLOCK, half)).T
            ref[j, BLOCK:, :] = spread[:MASS_ROWS].astype(jnp.bfloat16)


def shards(embed, values, match_frame, match_block, block_counts):
    frames = embed.shape[0]
    band_rows = embed.shape[1]
    half = embed.shape[2]
    blocks = band_rows // BLOCK
    hops = -(-REACH // frames)
    band_index = lax.axis_index("band")
    band_size = lax.axis_size("band")
    halo = 1 if band_size > 1 else 0
    chan_size = lax.axis_size("chan")
    chan_swap = [(i, (i + 1) % chan_size) for i in range(chan_size)]

    values_t = jnp.swapaxes(values.reshape(frames, blocks, BLOCK, half), -1, -2)
    features = jnp.concatenate([embed, values_t.reshape(frames, band_rows, half)], axis=2)
    if halo:
        features = with_halo(features, (("band", 1),), BLOCK)
    rimmed_blocks = blocks + 2 * halo
    per_slab = frames * rimmed_blocks
    window = []
    for offset in range(-hops, hops + 1):
        slab = features if offset == 0 else passed_along(features, "frame", -offset)
        window.append(slab.reshape(per_slab, BLOCK, 2 * half))
    others = [
        lax.ppermute(slab[:, :, :half], "chan", chan_swap) for slab in window
    ]
    slabs = len(window)
    center = hops * per_slab

    frame_ids = jnp.arange(frames, dtype=jnp.int32)
    key_rows = (hops * frames + frame_ids[:, None, None] + match_frame) * rimmed_blocks
    key_cols = match_block - band_index * blocks + halo
    slot = jnp.clip(key_rows + key_cols, 0, slabs * per_slab - 1).astype(jnp.int32).reshape(-1)
    block_ids = band_index * blocks + jnp.arange(blocks, dtype=jnp.int32)
    active = (block_ids[None, :] < block_counts[:, None]).astype(jnp.int32)
    queries = frames * blocks

    kernel = functools.partial(
        aggregate_kernel,
        slabs=slabs,
        per_slab=per_slab,
        center=center,
        queries=queries,
        half=half,
        blocks=blocks,
        rimmed=rimmed_blocks,
        halo=halo,
    )
    smem = pl.BlockSpec(memory_space=pltpu.SMEM)
    hbm = pl.BlockSpec(memory_space=pl.ANY)
    vmem = pl.BlockSpec(memory_space=pltpu.VMEM)
    out_shape = [
        jax.ShapeDtypeStruct((per_slab, BLOCK, half), jnp.float32),
        jax.ShapeDtypeStruct((per_slab, BLOCK, 1), jnp.float32),
    ] + [
        jax.ShapeDtypeStruct((per_slab, BLOCK + MASS_ROWS, half), jnp.bfloat16)
        for _ in range(slabs - 1)
    ]
    total = slabs * per_slab
    outs = pl.pallas_call(
        kernel,
        out_shape=out_shape,
        in_specs=[smem, smem] + [hbm] * (2 * slabs),
        out_specs=[vmem] * len(out_shape),
        scratch_shapes=[
            pltpu.VMEM((total, BLOCK, 2 * half), jnp.bfloat16),
            pltpu.VMEM((total, half, BLOCK), jnp.bfloat16),
            pltpu.VMEM((total, BLOCK, half), jnp.float32),
            pltpu.VMEM((total, BLOCK, 1), jnp.float32),
            pltpu.VMEM((2, K * BLOCK, 2 * half), jnp.bfloat16),
            pltpu.VMEM((2, half, K * BLOCK), jnp.bfloat16),
            pltpu.SemaphoreType.DMA((3, slabs)),
            pltpu.SemaphoreType.DMA((2, 2, K)),
        ],
    )(slot, active.reshape(-1), *window, *others)
    own_num, own_mass = outs[0], outs[1]
    remote = outs[2:]
    offsets = [o for o in range(-hops, hops + 1) if o != 0]
    for offset, outgoing in zip(offsets, remote):
        arrived = passed_along(outgoing, "frame", offset).astype(jnp.float32)
        own_num = own_num + arrived[:, :BLOCK, :]
        own_mass = own_mass + arrived[:, BLOCK, :][:, :, None]
    own_num = own_num.reshape(frames, rimmed_blocks, BLOCK, half)
    own_mass = own_mass.reshape(frames, rimmed_blocks, BLOCK)
    if halo:
        for toward in (1, -1):
            rim_block = blocks + 1 if toward > 0 else 0
            target_block = 1 if toward > 0 else blocks
            arrived = (
                passed_along(own_num[:, rim_block].astype(jnp.bfloat16), "band", toward).astype(
                    jnp.float32
                ),
                passed_along(own_mass[:, rim_block].astype(jnp.bfloat16), "band", toward).astype(
                    jnp.float32
                ),
            )
            own_num = own_num.at[:, target_block].add(arrived[0])
            own_mass = own_mass.at[:, target_block].add(arrived[1])
        own_num = own_num[:, 1 : blocks + 1]
        own_mass = own_mass[:, 1 : blocks + 1]
    numer = own_num
    value_blocks = values.reshape(frames, blocks, BLOCK, half).astype(jnp.float32)
    result = (numer + value_blocks) / (own_mass[..., None] + 1.0)
    return result.reshape(frames, band_rows, half).astype(jnp.bfloat16)


def solution(mesh):
    placed = (
        P(("reel", "frame"), "band", "chan"),
        P(("reel", "frame"), "band", "chan"),
        P(("reel", "frame"), "band", None),
        P(("reel", "frame"), "band", None),
        P(("reel", "frame")),
    )
    return jax.shard_map(
        shards,
        mesh=mesh,
        in_specs=placed,
        out_specs=P(("reel", "frame"), "band", "chan"),
        check_vma=False,
    )
```

```python
import functools
import math

import jax
import jax.numpy as jnp
from jax import lax
from jax.experimental import pallas as pl
from jax.experimental.pallas import tpu as pltpu
from jax.sharding import PartitionSpec as P

W = 256
BLOCK = 128
K = 16
REACH = 8
MASS_ROWS = 16


def with_halo(x, sides, width):
    for axis, dim in sides:
        size, length = (lax.axis_size(axis), x.shape[dim])
        up = [(i, (i + 1) % size) for i in range(size - 1)]
        down = [(j, i) for i, j in up]
        last = lax.slice_in_dim(x, length - width, length, axis=dim)
        initial = lax.slice_in_dim(x, 0, width, axis=dim)
        before = lax.ppermute(last, axis, up)
        after = lax.ppermute(initial, axis, down)
        x = jnp.concatenate([before, x, after], axis=dim)
    return x


def passed_along(block, axis, distance):
    devices = range(lax.axis_size(axis))
    route = [(i - distance, i) for i in devices if i - distance in devices]
    return lax.ppermute(block, axis, route)


def aggregate_kernel(
    slot_ref, act_ref, *refs, slabs, per_slab, center, queries, half, blocks, rimmed, halo
):
    sources = [refs[:slabs], refs[2 * slabs : 3 * slabs], refs[slabs : 2 * slabs]]
    own_num_ref, own_mass_ref = refs[3 * slabs : 3 * slabs + 2]
    remote_refs = refs[3 * slabs + 2 : 4 * slabs + 1]
    key_a, key_v, key_b, acc, macc, score_ref, sems = refs[4 * slabs + 1 :]

    copies = []
    for s in range(slabs):
        dst = pl.ds(s * per_slab, per_slab)
        for kind, target in enumerate((key_a, key_v, key_b)):
            copies.append(pltpu.make_async_copy(sources[kind][s], target.at[dst], sems.at[kind, s]))
    for c in copies:
        c.start()
    acc[...] = jnp.zeros(acc.shape, acc.dtype)
    macc[...] = jnp.zeros(macc.shape, macc.dtype)
    for c in copies:
        c.wait()

    score_scale = 1.0 / math.sqrt(W)
    dims_t = (((1,), (1,)), ((), ()))

    def one_query(i, carry):
        q_slot = center + (i // blocks) * rimmed + halo + i % blocks
        qa = key_a[q_slot]
        qb = key_b[q_slot]
        slots = [slot_ref[i * K + k] for k in range(K)]
        for k in range(K):
            s = slots[k]
            part = lax.dot_general(qa, key_a[s], dims_t, preferred_element_type=jnp.float32)
            part = part + lax.dot_general(qb, key_b[s], dims_t, preferred_element_type=jnp.float32)
            score_ref[:, k * BLOCK : (k + 1) * BLOCK] = part * score_scale
        score = score_ref[...]
        peak = jnp.max(score, axis=-1, keepdims=True)
        exponent = jnp.exp(score - peak)
        prob = exponent / jnp.sum(exponent, axis=-1, keepdims=True)
        attention = prob.astype(jnp.bfloat16)
        estimate = jnp.zeros((BLOCK, half), jnp.float32)
        for k in range(K):
            estimate = estimate + jnp.dot(
                attention[:, k * BLOCK : (k + 1) * BLOCK],
                key_v[slots[k]],
                preferred_element_type=jnp.float32,
            )
        estimate = estimate.astype(jnp.bfloat16).astype(jnp.float32)
        active = act_ref[i].astype(jnp.float32)
        masked = (attention.astype(jnp.float32) * active).astype(jnp.bfloat16)
        estimate_t = estimate.T.astype(jnp.bfloat16)
        contrib_t = jnp.dot(estimate_t, masked, preferred_element_type=jnp.float32)
        weights = jnp.sum(prob * active, axis=0, keepdims=True)
        for k in range(K):
            s = slots[k]
            acc[s] = acc[s] + contrib_t[:, k * BLOCK : (k + 1) * BLOCK]
            macc[s] = macc[s] + weights[:, k * BLOCK : (k + 1) * BLOCK]
        return carry

    lax.fori_loop(0, queries, one_query, 0)

    own = pl.ds(center, per_slab)
    own_num_ref[...] = acc[own]
    own_mass_ref[...] = macc[own]
    remote = [s for s in range(slabs) if s * per_slab != center]
    for ref, s in zip(remote_refs, remote):
        rows = pl.ds(s * per_slab, per_slab)
        ref[:, :half, :] = acc[rows].astype(jnp.bfloat16)
        ref[:, half:, :] = jnp.broadcast_to(macc[rows], (per_slab, MASS_ROWS, BLOCK)).astype(
            jnp.bfloat16
        )


def shards(embed, values, match_frame, match_block, block_counts):
    frames = embed.shape[0]
    band_rows = embed.shape[1]
    half = embed.shape[2]
    blocks = band_rows // BLOCK
    hops = -(-REACH // frames)
    band_index = lax.axis_index("band")
    band_size = lax.axis_size("band")
    halo = 1 if band_size > 1 else 0
    chan_size = lax.axis_size("chan")
    chan_swap = [(i, (i + 1) % chan_size) for i in range(chan_size)]

    if halo:
        embed, rim_values = (with_halo(x, (("band", 1),), BLOCK) for x in (embed, values))
    else:
        rim_values = values
    rimmed_blocks = blocks + 2 * halo
    per_slab = frames * rimmed_blocks
    window_e = []
    window_v = []
    for offset in range(-hops, hops + 1):
        for own, window in ((embed, window_e), (rim_values, window_v)):
            slab = own if offset == 0 else passed_along(own, "frame", -offset)
            window.append(slab.reshape(per_slab, BLOCK, half))
    others = [lax.ppermute(slab, "chan", chan_swap) for slab in window_e]
    slabs = len(window_e)
    center = hops * per_slab

    frame_ids = jnp.arange(frames, dtype=jnp.int32)
    key_rows = (hops * frames + frame_ids[:, None, None] + match_frame) * rimmed_blocks
    key_cols = match_block - band_index * blocks + halo
    slot = jnp.clip(key_rows + key_cols, 0, slabs * per_slab - 1).astype(jnp.int32).reshape(-1)
    block_ids = band_index * blocks + jnp.arange(blocks, dtype=jnp.int32)
    active = (block_ids[None, :] < block_counts[:, None]).astype(jnp.int32)
    queries = frames * blocks

    kernel = functools.partial(
        aggregate_kernel,
        slabs=slabs,
        per_slab=per_slab,
        center=center,
        queries=queries,
        half=half,
        blocks=blocks,
        rimmed=rimmed_blocks,
        halo=halo,
    )
    smem = pl.BlockSpec(memory_space=pltpu.SMEM)
    hbm = pl.BlockSpec(memory_space=pl.ANY)
    vmem = pl.BlockSpec(memory_space=pltpu.VMEM)
    out_shape = [
        jax.ShapeDtypeStruct((per_slab, half, BLOCK), jnp.float32),
        jax.ShapeDtypeStruct((per_slab, 1, BLOCK), jnp.float32),
    ] + [
        jax.ShapeDtypeStruct((per_slab, half + MASS_ROWS, BLOCK), jnp.bfloat16)
        for _ in range(slabs - 1)
    ]
    total = slabs * per_slab
    outs = pl.pallas_call(
        kernel,
        out_shape=out_shape,
        in_specs=[smem, smem] + [hbm] * (3 * slabs),
        out_specs=[vmem] * len(out_shape),
        scratch_shapes=[
            pltpu.VMEM((total, BLOCK, half), jnp.bfloat16),
            pltpu.VMEM((total, BLOCK, half), jnp.bfloat16),
            pltpu.VMEM((total, BLOCK, half), jnp.bfloat16),
            pltpu.VMEM((total, half, BLOCK), jnp.float32),
            pltpu.VMEM((total, 1, BLOCK), jnp.float32),
            pltpu.VMEM((BLOCK, K * BLOCK), jnp.float32),
            pltpu.SemaphoreType.DMA((3, slabs)),
        ],
    )(slot, active.reshape(-1), *window_e, *others, *window_v)
    own_num, own_mass = outs[0], outs[1]
    remote = outs[2:]
    offsets = [o for o in range(-hops, hops + 1) if o != 0]
    for offset, outgoing in zip(offsets, remote):
        arrived = passed_along(outgoing, "frame", offset).astype(jnp.float32)
        own_num = own_num + arrived[:, :half, :]
        own_mass = own_mass + arrived[:, half : half + 1, :]
    own_num = own_num.reshape(frames, rimmed_blocks, half, BLOCK)
    own_mass = own_mass.reshape(frames, rimmed_blocks, BLOCK)
    if halo:
        for toward in (1, -1):
            rim_block = blocks + 1 if toward > 0 else 0
            target_block = 1 if toward > 0 else blocks
            arrived = (
                passed_along(own_num[:, rim_block].astype(jnp.bfloat16), "band", toward).astype(
                    jnp.float32
                ),
                passed_along(own_mass[:, rim_block].astype(jnp.bfloat16), "band", toward).astype(
                    jnp.float32
                ),
            )
            own_num = own_num.at[:, target_block].add(arrived[0])
            own_mass = own_mass.at[:, target_block].add(arrived[1])
        own_num = own_num[:, 1 : blocks + 1]
        own_mass = own_mass[:, 1 : blocks + 1]
    numer = jnp.swapaxes(own_num, -1, -2)
    value_blocks = values.reshape(frames, blocks, BLOCK, half).astype(jnp.float32)
    result = (numer + value_blocks) / (own_mass[..., None] + 1.0)
    return result.reshape(frames, band_rows, half).astype(jnp.bfloat16)


def solution(mesh):
    placed = (
        P(("reel", "frame"), "band", "chan"),
        P(("reel", "frame"), "band", "chan"),
        P(("reel", "frame"), "band", None),
        P(("reel", "frame"), "band", None),
        P(("reel", "frame")),
    )
    return jax.shard_map(
        shards,
        mesh=mesh,
        in_specs=placed,
        out_specs=P(("reel", "frame"), "band", "chan"),
        check_vma=False,
    )
```

```python
import functools
import math

import jax
import jax.numpy as jnp
from jax import lax
from jax.experimental import pallas as pl
from jax.experimental.pallas import tpu as pltpu
from jax.sharding import PartitionSpec as P

W = 256
BLOCK = 128
K = 16
REACH = 8
MASS_ROWS = 16


def with_halo(x, sides, width):
    for axis, dim in sides:
        size, length = (lax.axis_size(axis), x.shape[dim])
        up = [(i, (i + 1) % size) for i in range(size - 1)]
        down = [(j, i) for i, j in up]
        last = lax.slice_in_dim(x, length - width, length, axis=dim)
        initial = lax.slice_in_dim(x, 0, width, axis=dim)
        before = lax.ppermute(last, axis, up)
        after = lax.ppermute(initial, axis, down)
        x = jnp.concatenate([before, x, after], axis=dim)
    return x


def passed_along(block, axis, distance):
    devices = range(lax.axis_size(axis))
    route = [(i - distance, i) for i in devices if i - distance in devices]
    return lax.ppermute(block, axis, route)


def score_kernel(slot_ref, act_ref, *refs, slabs, per_slab, center, queries, blocks, rimmed, halo):
    sources = [refs[:slabs], refs[slabs : 2 * slabs]]
    att_ref, mass_ref = refs[2 * slabs : 2 * slabs + 2]
    key_a, key_b, score_ref, sems = refs[2 * slabs + 2 :]

    copies = []
    for s in range(slabs):
        dst = pl.ds(s * per_slab, per_slab)
        for kind, target in enumerate((key_a, key_b)):
            copies.append(pltpu.make_async_copy(sources[kind][s], target.at[dst], sems.at[kind, s]))
    for c in copies:
        c.start()
    mass_ref[...] = jnp.zeros(mass_ref.shape, mass_ref.dtype)
    for c in copies:
        c.wait()

    score_scale = 1.0 / math.sqrt(W)
    dims_t = (((1,), (1,)), ((), ()))

    def one_query(i, carry):
        q_slot = center + (i // blocks) * rimmed + halo + i % blocks
        qa = key_a[q_slot]
        qb = key_b[q_slot]
        slots = [slot_ref[i * K + k] for k in range(K)]
        for k in range(K):
            s = slots[k]
            part = lax.dot_general(qa, key_a[s], dims_t, preferred_element_type=jnp.float32)
            part = part + lax.dot_general(qb, key_b[s], dims_t, preferred_element_type=jnp.float32)
            score_ref[:, k * BLOCK : (k + 1) * BLOCK] = part * score_scale
        score = score_ref[...]
        peak = jnp.max(score, axis=-1, keepdims=True)
        exponent = jnp.exp(score - peak)
        prob = exponent / jnp.sum(exponent, axis=-1, keepdims=True)
        att_ref[i] = prob.astype(jnp.bfloat16)
        active = act_ref[i].astype(jnp.float32)
        weights = jnp.sum(prob * active, axis=0, keepdims=True)
        for k in range(K):
            s = slots[k]
            mass_ref[s] = mass_ref[s] + weights[:, k * BLOCK : (k + 1) * BLOCK]
        return carry

    lax.fori_loop(0, queries, one_query, 0)


def value_kernel(slot_ref, act_ref, *refs, slabs, per_slab, center, queries, half):
    sources = refs[:slabs]
    att_ref, mass_ref = refs[slabs : slabs + 2]
    own_num_ref, own_mass_ref = refs[slabs + 2 : slabs + 4]
    remote_refs = refs[slabs + 4 : 2 * slabs + 3]
    key_v, acc, sems = refs[2 * slabs + 3 :]

    copies = []
    for s in range(slabs):
        dst = pl.ds(s * per_slab, per_slab)
        copies.append(pltpu.make_async_copy(sources[s], key_v.at[dst], sems.at[s]))
    for c in copies:
        c.start()
    acc[...] = jnp.zeros(acc.shape, acc.dtype)
    for c in copies:
        c.wait()

    def one_query(i, carry):
        slots = [slot_ref[i * K + k] for k in range(K)]
        attention = att_ref[i]
        estimate = jnp.zeros((BLOCK, half), jnp.float32)
        for k in range(K):
            estimate = estimate + jnp.dot(
                attention[:, k * BLOCK : (k + 1) * BLOCK],
                key_v[slots[k]],
                preferred_element_type=jnp.float32,
            )
        estimate = estimate.astype(jnp.bfloat16).astype(jnp.float32)
        active = act_ref[i].astype(jnp.float32)
        masked = (attention.astype(jnp.float32) * active).astype(jnp.bfloat16)
        estimate_t = estimate.T.astype(jnp.bfloat16)
        contrib_t = jnp.dot(estimate_t, masked, preferred_element_type=jnp.float32)
        for k in range(K):
            s = slots[k]
            acc[s] = acc[s] + contrib_t[:, k * BLOCK : (k + 1) * BLOCK]
        return carry

    lax.fori_loop(0, queries, one_query, 0)

    own = pl.ds(center, per_slab)
    own_num_ref[...] = acc[own]
    own_mass_ref[...] = mass_ref[own]
    remote = [s for s in range(slabs) if s * per_slab != center]
    for ref, s in zip(remote_refs, remote):
        rows = pl.ds(s * per_slab, per_slab)
        ref[:, :half, :] = acc[rows].astype(jnp.bfloat16)
        ref[:, half:, :] = jnp.broadcast_to(mass_ref[rows], (per_slab, MASS_ROWS, BLOCK)).astype(
            jnp.bfloat16
        )


def shards(embed, values, match_frame, match_block, block_counts):
    frames = embed.shape[0]
    band_rows = embed.shape[1]
    half = embed.shape[2]
    blocks = band_rows // BLOCK
    hops = -(-REACH // frames)
    band_index = lax.axis_index("band")
    band_size = lax.axis_size("band")
    halo = 1 if band_size > 1 else 0
    chan_size = lax.axis_size("chan")
    chan_swap = [(i, (i + 1) % chan_size) for i in range(chan_size)]

    if halo:
        embed, rim_values = (with_halo(x, (("band", 1),), BLOCK) for x in (embed, values))
    else:
        rim_values = values
    rimmed_blocks = blocks + 2 * halo
    per_slab = frames * rimmed_blocks
    window_e = []
    window_v = []
    for own, window in ((embed, window_e), (rim_values, window_v)):
        for offset in range(-hops, hops + 1):
            slab = own if offset == 0 else passed_along(own, "frame", -offset)
            window.append(slab.reshape(per_slab, BLOCK, half))
    others = [lax.ppermute(slab, "chan", chan_swap) for slab in window_e]
    slabs = len(window_e)
    center = hops * per_slab

    frame_ids = jnp.arange(frames, dtype=jnp.int32)
    key_rows = (hops * frames + frame_ids[:, None, None] + match_frame) * rimmed_blocks
    key_cols = match_block - band_index * blocks + halo
    slot = jnp.clip(key_rows + key_cols, 0, slabs * per_slab - 1).astype(jnp.int32).reshape(-1)
    block_ids = band_index * blocks + jnp.arange(blocks, dtype=jnp.int32)
    active = (block_ids[None, :] < block_counts[:, None]).astype(jnp.int32)
    queries = frames * blocks

    smem = pl.BlockSpec(memory_space=pltpu.SMEM)
    hbm = pl.BlockSpec(memory_space=pl.ANY)
    vmem = pl.BlockSpec(memory_space=pltpu.VMEM)
    total = slabs * per_slab
    gates = active.reshape(-1)
    attention, mass = pl.pallas_call(
        functools.partial(
            score_kernel,
            slabs=slabs,
            per_slab=per_slab,
            center=center,
            queries=queries,
            blocks=blocks,
            rimmed=rimmed_blocks,
            halo=halo,
        ),
        out_shape=[
            jax.ShapeDtypeStruct((queries, BLOCK, K * BLOCK), jnp.bfloat16),
            jax.ShapeDtypeStruct((total, 1, BLOCK), jnp.float32),
        ],
        in_specs=[smem, smem] + [hbm] * (2 * slabs),
        out_specs=[vmem, vmem],
        scratch_shapes=[
            pltpu.VMEM((total, BLOCK, half), jnp.bfloat16),
            pltpu.VMEM((total, BLOCK, half), jnp.bfloat16),
            pltpu.VMEM((BLOCK, K * BLOCK), jnp.float32),
            pltpu.SemaphoreType.DMA((2, slabs)),
        ],
    )(slot, gates, *window_e, *others)
    out_shape = [
        jax.ShapeDtypeStruct((per_slab, half, BLOCK), jnp.float32),
        jax.ShapeDtypeStruct((per_slab, 1, BLOCK), jnp.float32),
    ] + [
        jax.ShapeDtypeStruct((per_slab, half + MASS_ROWS, BLOCK), jnp.bfloat16)
        for _ in range(slabs - 1)
    ]
    outs = pl.pallas_call(
        functools.partial(
            value_kernel,
            slabs=slabs,
            per_slab=per_slab,
            center=center,
            queries=queries,
            half=half,
        ),
        out_shape=out_shape,
        in_specs=[smem, smem] + [hbm] * slabs + [vmem, vmem],
        out_specs=[vmem] * len(out_shape),
        scratch_shapes=[
            pltpu.VMEM((total, BLOCK, half), jnp.bfloat16),
            pltpu.VMEM((total, half, BLOCK), jnp.float32),
            pltpu.SemaphoreType.DMA((slabs,)),
        ],
    )(slot, gates, *window_v, attention, mass)
    own_num, own_mass = outs[0], outs[1]
    remote = outs[2:]
    offsets = [o for o in range(-hops, hops + 1) if o != 0]
    for offset, outgoing in zip(offsets, remote):
        arrived = passed_along(outgoing, "frame", offset).astype(jnp.float32)
        own_num = own_num + arrived[:, :half, :]
        own_mass = own_mass + arrived[:, half : half + 1, :]
    own_num = own_num.reshape(frames, rimmed_blocks, half, BLOCK)
    own_mass = own_mass.reshape(frames, rimmed_blocks, BLOCK)
    if halo:
        for toward in (1, -1):
            rim_block = blocks + 1 if toward > 0 else 0
            target_block = 1 if toward > 0 else blocks
            arrived = (
                passed_along(own_num[:, rim_block].astype(jnp.bfloat16), "band", toward).astype(
                    jnp.float32
                ),
                passed_along(own_mass[:, rim_block].astype(jnp.bfloat16), "band", toward).astype(
                    jnp.float32
                ),
            )
            own_num = own_num.at[:, target_block].add(arrived[0])
            own_mass = own_mass.at[:, target_block].add(arrived[1])
        own_num = own_num[:, 1 : blocks + 1]
        own_mass = own_mass[:, 1 : blocks + 1]
    numer = jnp.swapaxes(own_num, -1, -2)
    value_blocks = values.reshape(frames, blocks, BLOCK, half).astype(jnp.float32)
    result = (numer + value_blocks) / (own_mass[..., None] + 1.0)
    return result.reshape(frames, band_rows, half).astype(jnp.bfloat16)


def solution(mesh):
    placed = (
        P(("reel", "frame"), "band", "chan"),
        P(("reel", "frame"), "band", "chan"),
        P(("reel", "frame"), "band", None),
        P(("reel", "frame"), "band", None),
        P(("reel", "frame")),
    )
    return jax.shard_map(
        shards,
        mesh=mesh,
        in_specs=placed,
        out_specs=P(("reel", "frame"), "band", "chan"),
        check_vma=False,
    )
```

```python
import functools
import math

import jax
import jax.numpy as jnp
from jax import lax
from jax.experimental import pallas as pl
from jax.experimental.pallas import tpu as pltpu
from jax.sharding import PartitionSpec as P

W = 256
BLOCK = 128
K = 16
REACH = 8
MASS_ROWS = 16


def with_halo(x, sides, width):
    for axis, dim in sides:
        size, length = (lax.axis_size(axis), x.shape[dim])
        up = [(i, (i + 1) % size) for i in range(size - 1)]
        down = [(j, i) for i, j in up]
        last = lax.slice_in_dim(x, length - width, length, axis=dim)
        initial = lax.slice_in_dim(x, 0, width, axis=dim)
        before = lax.ppermute(last, axis, up)
        after = lax.ppermute(initial, axis, down)
        x = jnp.concatenate([before, x, after], axis=dim)
    return x


def passed_along(block, axis, distance):
    devices = range(lax.axis_size(axis))
    route = [(i - distance, i) for i in devices if i - distance in devices]
    return lax.ppermute(block, axis, route)


def aggregate_kernel(
    slot_ref, act_ref, *refs, slabs, per_slab, center, queries, half, blocks, rimmed, halo
):
    sources = [refs[:slabs], refs[2 * slabs : 3 * slabs], refs[slabs : 2 * slabs]]
    own_num_ref, own_mass_ref = refs[3 * slabs : 3 * slabs + 2]
    remote_refs = refs[3 * slabs + 2 : 4 * slabs + 1]
    key_e, key_v, acc, macc, score_ref, value_ref, sems = refs[4 * slabs + 1 :]

    copies = []
    for s in range(slabs):
        dst = pl.ds(s * per_slab, per_slab)
        targets = (
            key_e.at[dst, :, pl.ds(0, half)],
            key_v.at[dst],
            key_e.at[dst, :, pl.ds(half, half)],
        )
        for kind, target in enumerate(targets):
            copies.append(pltpu.make_async_copy(sources[kind][s], target, sems.at[kind, s]))
    for c in copies:
        c.start()
    acc[...] = jnp.zeros(acc.shape, acc.dtype)
    macc[...] = jnp.zeros(macc.shape, macc.dtype)
    for c in copies:
        c.wait()

    score_scale = 1.0 / math.sqrt(W)
    dims_t = (((1,), (1,)), ((), ()))

    def one_query(i, carry):
        q_slot = center + (i // blocks) * rimmed + halo + i % blocks
        query = key_e[q_slot]
        slots = [slot_ref[i * K + k] for k in range(K)]
        for k in range(K):
            s = slots[k]
            part = lax.dot_general(query, key_e[s], dims_t, preferred_element_type=jnp.float32)
            score_ref[:, k * BLOCK : (k + 1) * BLOCK] = part * score_scale
            value_ref[k * BLOCK : (k + 1) * BLOCK, :] = key_v[s]
        score = score_ref[...]
        peak = jnp.max(score, axis=-1, keepdims=True)
        exponent = jnp.exp(score - peak)
        prob = exponent / jnp.sum(exponent, axis=-1, keepdims=True)
        attention = prob.astype(jnp.bfloat16)
        estimate = jnp.dot(attention, value_ref[...], preferred_element_type=jnp.float32)
        estimate = estimate.astype(jnp.bfloat16).astype(jnp.float32)
        active = act_ref[i].astype(jnp.float32)
        masked = (attention.astype(jnp.float32) * active).astype(jnp.bfloat16)
        estimate_t = estimate.T.astype(jnp.bfloat16)
        contrib_t = jnp.dot(estimate_t, masked, preferred_element_type=jnp.float32)
        weights = jnp.sum(prob * active, axis=0, keepdims=True)
        for k in range(K):
            s = slots[k]
            acc[s] = acc[s] + contrib_t[:, k * BLOCK : (k + 1) * BLOCK]
            macc[s] = macc[s] + weights[:, k * BLOCK : (k + 1) * BLOCK]
        return carry

    lax.fori_loop(0, queries, one_query, 0)

    own = pl.ds(center, per_slab)
    own_num_ref[...] = acc[own]
    own_mass_ref[...] = macc[own]
    remote = [s for s in range(slabs) if s * per_slab != center]
    for ref, s in zip(remote_refs, remote):
        rows = pl.ds(s * per_slab, per_slab)
        ref[:, :half, :] = acc[rows].astype(jnp.bfloat16)
        ref[:, half:, :] = jnp.broadcast_to(macc[rows], (per_slab, MASS_ROWS, BLOCK)).astype(
            jnp.bfloat16
        )


def shards(embed, values, match_frame, match_block, block_counts):
    frames = embed.shape[0]
    band_rows = embed.shape[1]
    half = embed.shape[2]
    blocks = band_rows // BLOCK
    hops = -(-REACH // frames)
    band_index = lax.axis_index("band")
    band_size = lax.axis_size("band")
    halo = 1 if band_size > 1 else 0
    chan_size = lax.axis_size("chan")
    chan_swap = [(i, (i + 1) % chan_size) for i in range(chan_size)]

    if halo:
        embed, rim_values = (with_halo(x, (("band", 1),), BLOCK) for x in (embed, values))
    else:
        rim_values = values
    rimmed_blocks = blocks + 2 * halo
    per_slab = frames * rimmed_blocks
    window_e = []
    window_v = []
    for offset in range(-hops, hops + 1):
        for own, window in ((embed, window_e), (rim_values, window_v)):
            slab = own if offset == 0 else passed_along(own, "frame", -offset)
            window.append(slab.reshape(per_slab, BLOCK, half))
    others = [lax.ppermute(slab, "chan", chan_swap) for slab in window_e]
    slabs = len(window_e)
    center = hops * per_slab

    frame_ids = jnp.arange(frames, dtype=jnp.int32)
    key_rows = (hops * frames + frame_ids[:, None, None] + match_frame) * rimmed_blocks
    key_cols = match_block - band_index * blocks + halo
    slot = jnp.clip(key_rows + key_cols, 0, slabs * per_slab - 1).astype(jnp.int32).reshape(-1)
    block_ids = band_index * blocks + jnp.arange(blocks, dtype=jnp.int32)
    active = (block_ids[None, :] < block_counts[:, None]).astype(jnp.int32)
    queries = frames * blocks

    kernel = functools.partial(
        aggregate_kernel,
        slabs=slabs,
        per_slab=per_slab,
        center=center,
        queries=queries,
        half=half,
        blocks=blocks,
        rimmed=rimmed_blocks,
        halo=halo,
    )
    smem = pl.BlockSpec(memory_space=pltpu.SMEM)
    hbm = pl.BlockSpec(memory_space=pl.ANY)
    vmem = pl.BlockSpec(memory_space=pltpu.VMEM)
    out_shape = [
        jax.ShapeDtypeStruct((per_slab, half, BLOCK), jnp.float32),
        jax.ShapeDtypeStruct((per_slab, 1, BLOCK), jnp.float32),
    ] + [
        jax.ShapeDtypeStruct((per_slab, half + MASS_ROWS, BLOCK), jnp.bfloat16)
        for _ in range(slabs - 1)
    ]
    total = slabs * per_slab
    outs = pl.pallas_call(
        kernel,
        out_shape=out_shape,
        in_specs=[smem, smem] + [hbm] * (3 * slabs),
        out_specs=[vmem] * len(out_shape),
        scratch_shapes=[
            pltpu.VMEM((total, BLOCK, 2 * half), jnp.bfloat16),
            pltpu.VMEM((total, BLOCK, half), jnp.bfloat16),
            pltpu.VMEM((total, half, BLOCK), jnp.float32),
            pltpu.VMEM((total, 1, BLOCK), jnp.float32),
            pltpu.VMEM((BLOCK, K * BLOCK), jnp.float32),
            pltpu.VMEM((K * BLOCK, half), jnp.bfloat16),
            pltpu.SemaphoreType.DMA((3, slabs)),
        ],
    )(slot, active.reshape(-1), *window_e, *others, *window_v)
    own_num, own_mass = outs[0], outs[1]
    remote = outs[2:]
    offsets = [o for o in range(-hops, hops + 1) if o != 0]
    for offset, outgoing in zip(offsets, remote):
        arrived = passed_along(outgoing, "frame", offset).astype(jnp.float32)
        own_num = own_num + arrived[:, :half, :]
        own_mass = own_mass + arrived[:, half : half + 1, :]
    own_num = own_num.reshape(frames, rimmed_blocks, half, BLOCK)
    own_mass = own_mass.reshape(frames, rimmed_blocks, BLOCK)
    if halo:
        for toward in (1, -1):
            rim_block = blocks + 1 if toward > 0 else 0
            target_block = 1 if toward > 0 else blocks
            arrived = (
                passed_along(own_num[:, rim_block].astype(jnp.bfloat16), "band", toward).astype(
                    jnp.float32
                ),
                passed_along(own_mass[:, rim_block].astype(jnp.bfloat16), "band", toward).astype(
                    jnp.float32
                ),
            )
            own_num = own_num.at[:, target_block].add(arrived[0])
            own_mass = own_mass.at[:, target_block].add(arrived[1])
        own_num = own_num[:, 1 : blocks + 1]
        own_mass = own_mass[:, 1 : blocks + 1]
    numer = jnp.swapaxes(own_num, -1, -2)
    value_blocks = values.reshape(frames, blocks, BLOCK, half).astype(jnp.float32)
    result = (numer + value_blocks) / (own_mass[..., None] + 1.0)
    return result.reshape(frames, band_rows, half).astype(jnp.bfloat16)


def solution(mesh):
    placed = (
        P(("reel", "frame"), "band", "chan"),
        P(("reel", "frame"), "band", "chan"),
        P(("reel", "frame"), "band", None),
        P(("reel", "frame"), "band", None),
        P(("reel", "frame")),
    )
    return jax.shard_map(
        shards,
        mesh=mesh,
        in_specs=placed,
        out_specs=P(("reel", "frame"), "band", "chan"),
        check_vma=False,
    )
```

```python
import functools
import math

import jax
import jax.numpy as jnp
from jax import lax
from jax.experimental import pallas as pl
from jax.experimental.pallas import tpu as pltpu
from jax.sharding import PartitionSpec as P

W = 256
BLOCK = 128
K = 16
REACH = 8
MASS_ROWS = 16


def with_halo(x, sides, width):
    for axis, dim in sides:
        size, length = (lax.axis_size(axis), x.shape[dim])
        up = [(i, (i + 1) % size) for i in range(size - 1)]
        down = [(j, i) for i, j in up]
        last = lax.slice_in_dim(x, length - width, length, axis=dim)
        initial = lax.slice_in_dim(x, 0, width, axis=dim)
        before = lax.ppermute(last, axis, up)
        after = lax.ppermute(initial, axis, down)
        x = jnp.concatenate([before, x, after], axis=dim)
    return x


def passed_along(block, axis, distance):
    devices = range(lax.axis_size(axis))
    route = [(i - distance, i) for i in devices if i - distance in devices]
    return lax.ppermute(block, axis, route)


def aggregate_kernel(
    slot_ref, act_ref, *refs, slabs, per_slab, center, queries, half, blocks, rimmed, halo
):
    sources = [refs[:slabs], refs[2 * slabs : 3 * slabs], refs[slabs : 2 * slabs]]
    own_num_ref, own_mass_ref = refs[3 * slabs : 3 * slabs + 2]
    remote_refs = refs[3 * slabs + 2 : 4 * slabs + 1]
    key_e, key_v, acc, macc, score_ref, value_ref, sems = refs[4 * slabs + 1 :]

    copies = []
    for s in range(slabs):
        dst = pl.ds(s * per_slab, per_slab)
        targets = (
            key_e.at[dst, :, pl.ds(0, half)],
            key_v.at[dst],
            key_e.at[dst, :, pl.ds(half, half)],
        )
        for kind, target in enumerate(targets):
            copies.append(pltpu.make_async_copy(sources[kind][s], target, sems.at[kind, s]))
    for c in copies:
        c.start()
    acc[...] = jnp.zeros(acc.shape, acc.dtype)
    macc[...] = jnp.zeros(macc.shape, macc.dtype)
    for c in copies:
        c.wait()

    score_scale = 1.0 / math.sqrt(W)
    dims_t = (((1,), (1,)), ((), ()))

    def one_query(i, carry):
        q_slot = center + (i // blocks) * rimmed + halo + i % blocks
        query = key_e[q_slot] * jnp.asarray(score_scale, jnp.bfloat16)
        slots = [slot_ref[i * K + k] for k in range(K)]
        for k in range(K):
            s = slots[k]
            part = lax.dot_general(query, key_e[s], dims_t, preferred_element_type=jnp.float32)
            score_ref[:, k * BLOCK : (k + 1) * BLOCK] = part
            value_ref[k * BLOCK : (k + 1) * BLOCK, :] = key_v[s]
        score = score_ref[...]
        peak = jnp.max(score, axis=-1, keepdims=True)
        exponent = jnp.exp(score - peak)
        prob = exponent / jnp.sum(exponent, axis=-1, keepdims=True)
        attention = prob.astype(jnp.bfloat16)
        estimate = jnp.dot(attention, value_ref[...], preferred_element_type=jnp.float32)
        active = act_ref[i].astype(jnp.float32)
        estimate = estimate.astype(jnp.bfloat16).astype(jnp.float32) * active
        estimate_t = estimate.T.astype(jnp.bfloat16)
        contrib_t = jnp.dot(estimate_t, attention, preferred_element_type=jnp.float32)
        weights = jnp.sum(prob, axis=0, keepdims=True) * active
        for k in range(K):
            s = slots[k]
            acc[s] = acc[s] + contrib_t[:, k * BLOCK : (k + 1) * BLOCK]
            macc[s] = macc[s] + weights[:, k * BLOCK : (k + 1) * BLOCK]
        return carry

    lax.fori_loop(0, queries, one_query, 0)

    own = pl.ds(center, per_slab)
    own_num_ref[...] = acc[own]
    own_mass_ref[...] = macc[own]
    remote = [s for s in range(slabs) if s * per_slab != center]
    for ref, s in zip(remote_refs, remote):
        rows = pl.ds(s * per_slab, per_slab)
        ref[:, :half, :] = acc[rows].astype(jnp.bfloat16)
        ref[:, half:, :] = jnp.broadcast_to(macc[rows], (per_slab, MASS_ROWS, BLOCK)).astype(
            jnp.bfloat16
        )


def shards(embed, values, match_frame, match_block, block_counts):
    frames = embed.shape[0]
    band_rows = embed.shape[1]
    half = embed.shape[2]
    blocks = band_rows // BLOCK
    hops = -(-REACH // frames)
    band_index = lax.axis_index("band")
    band_size = lax.axis_size("band")
    halo = 1 if band_size > 1 else 0
    chan_size = lax.axis_size("chan")
    chan_swap = [(i, (i + 1) % chan_size) for i in range(chan_size)]

    if halo:
        embed, rim_values = (with_halo(x, (("band", 1),), BLOCK) for x in (embed, values))
    else:
        rim_values = values
    rimmed_blocks = blocks + 2 * halo
    per_slab = frames * rimmed_blocks
    window_e = []
    window_v = []
    for offset in range(-hops, hops + 1):
        for own, window in ((embed, window_e), (rim_values, window_v)):
            slab = own if offset == 0 else passed_along(own, "frame", -offset)
            window.append(slab.reshape(per_slab, BLOCK, half))
    others = [lax.ppermute(slab, "chan", chan_swap) for slab in window_e]
    slabs = len(window_e)
    center = hops * per_slab

    frame_ids = jnp.arange(frames, dtype=jnp.int32)
    key_rows = (hops * frames + frame_ids[:, None, None] + match_frame) * rimmed_blocks
    key_cols = match_block - band_index * blocks + halo
    slot = jnp.clip(key_rows + key_cols, 0, slabs * per_slab - 1).astype(jnp.int32).reshape(-1)
    block_ids = band_index * blocks + jnp.arange(blocks, dtype=jnp.int32)
    active = (block_ids[None, :] < block_counts[:, None]).astype(jnp.int32)
    queries = frames * blocks

    kernel = functools.partial(
        aggregate_kernel,
        slabs=slabs,
        per_slab=per_slab,
        center=center,
        queries=queries,
        half=half,
        blocks=blocks,
        rimmed=rimmed_blocks,
        halo=halo,
    )
    smem = pl.BlockSpec(memory_space=pltpu.SMEM)
    hbm = pl.BlockSpec(memory_space=pl.ANY)
    vmem = pl.BlockSpec(memory_space=pltpu.VMEM)
    out_shape = [
        jax.ShapeDtypeStruct((per_slab, half, BLOCK), jnp.float32),
        jax.ShapeDtypeStruct((per_slab, 1, BLOCK), jnp.float32),
    ] + [
        jax.ShapeDtypeStruct((per_slab, half + MASS_ROWS, BLOCK), jnp.bfloat16)
        for _ in range(slabs - 1)
    ]
    total = slabs * per_slab
    outs = pl.pallas_call(
        kernel,
        out_shape=out_shape,
        in_specs=[smem, smem] + [hbm] * (3 * slabs),
        out_specs=[vmem] * len(out_shape),
        scratch_shapes=[
            pltpu.VMEM((total, BLOCK, 2 * half), jnp.bfloat16),
            pltpu.VMEM((total, BLOCK, half), jnp.bfloat16),
            pltpu.VMEM((total, half, BLOCK), jnp.float32),
            pltpu.VMEM((total, 1, BLOCK), jnp.float32),
            pltpu.VMEM((BLOCK, K * BLOCK), jnp.float32),
            pltpu.VMEM((K * BLOCK, half), jnp.bfloat16),
            pltpu.SemaphoreType.DMA((3, slabs)),
        ],
    )(slot, active.reshape(-1), *window_e, *others, *window_v)
    own_num, own_mass = outs[0], outs[1]
    remote = outs[2:]
    offsets = [o for o in range(-hops, hops + 1) if o != 0]
    for offset, outgoing in zip(offsets, remote):
        arrived = passed_along(outgoing, "frame", offset).astype(jnp.float32)
        own_num = own_num + arrived[:, :half, :]
        own_mass = own_mass + arrived[:, half : half + 1, :]
    own_num = own_num.reshape(frames, rimmed_blocks, half, BLOCK)
    own_mass = own_mass.reshape(frames, rimmed_blocks, BLOCK)
    if halo:
        for toward in (1, -1):
            rim_block = blocks + 1 if toward > 0 else 0
            target_block = 1 if toward > 0 else blocks
            arrived = (
                passed_along(own_num[:, rim_block].astype(jnp.bfloat16), "band", toward).astype(
                    jnp.float32
                ),
                passed_along(own_mass[:, rim_block].astype(jnp.bfloat16), "band", toward).astype(
                    jnp.float32
                ),
            )
            own_num = own_num.at[:, target_block].add(arrived[0])
            own_mass = own_mass.at[:, target_block].add(arrived[1])
        own_num = own_num[:, 1 : blocks + 1]
        own_mass = own_mass[:, 1 : blocks + 1]
    numer = jnp.swapaxes(own_num, -1, -2)
    value_blocks = values.reshape(frames, blocks, BLOCK, half).astype(jnp.float32)
    result = (numer + value_blocks) / (own_mass[..., None] + 1.0)
    return result.reshape(frames, band_rows, half).astype(jnp.bfloat16)


def solution(mesh):
    placed = (
        P(("reel", "frame"), "band", "chan"),
        P(("reel", "frame"), "band", "chan"),
        P(("reel", "frame"), "band", None),
        P(("reel", "frame"), "band", None),
        P(("reel", "frame")),
    )
    return jax.shard_map(
        shards,
        mesh=mesh,
        in_specs=placed,
        out_specs=P(("reel", "frame"), "band", "chan"),
        check_vma=False,
    )
```

```python
import functools
import math

import jax
import jax.numpy as jnp
from jax import lax
from jax.experimental import pallas as pl
from jax.experimental.pallas import tpu as pltpu
from jax.sharding import PartitionSpec as P

W = 256
BLOCK = 128
K = 16
REACH = 8
MASS_ROWS = 16


def with_halo(x, sides, width):
    for axis, dim in sides:
        size, length = (lax.axis_size(axis), x.shape[dim])
        up = [(i, (i + 1) % size) for i in range(size - 1)]
        down = [(j, i) for i, j in up]
        last = lax.slice_in_dim(x, length - width, length, axis=dim)
        initial = lax.slice_in_dim(x, 0, width, axis=dim)
        before = lax.ppermute(last, axis, up)
        after = lax.ppermute(initial, axis, down)
        x = jnp.concatenate([before, x, after], axis=dim)
    return x


def passed_along(block, axis, distance):
    devices = range(lax.axis_size(axis))
    route = [(i - distance, i) for i in devices if i - distance in devices]
    return lax.ppermute(block, axis, route)


def aggregate_kernel(
    slot_ref, act_ref, *refs, slabs, per_slab, center, queries, half, blocks, rimmed, halo
):
    sources = [refs[:slabs], refs[2 * slabs : 3 * slabs], refs[slabs : 2 * slabs]]
    own_num_ref, own_mass_ref = refs[3 * slabs : 3 * slabs + 2]
    remote_refs = refs[3 * slabs + 2 : 4 * slabs + 1]
    key_e, key_v, acc, macc, score_ref, value_ref, sems = refs[4 * slabs + 1 :]

    copies = []
    for s in range(slabs):
        dst = pl.ds(s * per_slab, per_slab)
        targets = (
            key_e.at[dst, :, pl.ds(0, half)],
            key_v.at[dst],
            key_e.at[dst, :, pl.ds(half, half)],
        )
        for kind, target in enumerate(targets):
            copies.append(pltpu.make_async_copy(sources[kind][s], target, sems.at[kind, s]))
    for c in copies:
        c.start()
    acc[...] = jnp.zeros(acc.shape, acc.dtype)
    macc[...] = jnp.zeros(macc.shape, macc.dtype)
    for c in copies:
        c.wait()

    score_scale = 1.0 / math.sqrt(W)
    dims_t = (((1,), (1,)), ((), ()))

    def one_query(i, carry):
        q_slot = center + (i // blocks) * rimmed + halo + i % blocks
        query = key_e[q_slot] * jnp.asarray(score_scale, jnp.bfloat16)
        slots = [slot_ref[i * K + k] for k in range(K)]
        for k in range(K):
            s = slots[k]
            part = lax.dot_general(query, key_e[s], dims_t, preferred_element_type=jnp.float32)
            score_ref[:, k * BLOCK : (k + 1) * BLOCK] = part
            value_ref[k * BLOCK : (k + 1) * BLOCK, :] = key_v[s]
        score = score_ref[...]
        peak = jnp.max(score, axis=-1, keepdims=True)
        exponent = jnp.exp(score - peak)
        prob = exponent / jnp.sum(exponent, axis=-1, keepdims=True)
        attention = prob.astype(jnp.bfloat16)
        estimate = jnp.dot(attention, value_ref[...], preferred_element_type=jnp.float32)
        active = act_ref[i].astype(jnp.float32)
        estimate = estimate.astype(jnp.bfloat16).astype(jnp.float32) * active
        estimate_t = estimate.T.astype(jnp.bfloat16)
        contrib_t = jnp.dot(estimate_t, attention, preferred_element_type=jnp.float32)
        weights = jnp.sum(prob, axis=0, keepdims=True) * active
        for k in range(K):
            s = slots[k]
            acc[s] = acc[s] + contrib_t[:, k * BLOCK : (k + 1) * BLOCK]
            macc[s] = macc[s] + weights[:, k * BLOCK : (k + 1) * BLOCK]
        return carry

    lax.fori_loop(0, queries, one_query, 0)

    own = pl.ds(center, per_slab)
    own_num_ref[...] = acc[own]
    own_mass_ref[...] = macc[own]
    remote = [s for s in range(slabs) if s * per_slab != center]
    for ref, s in zip(remote_refs, remote):
        rows = pl.ds(s * per_slab, per_slab)
        ref[:, :half, :] = acc[rows].astype(jnp.bfloat16)
        ref[:, half:, :] = jnp.broadcast_to(macc[rows], (per_slab, MASS_ROWS, BLOCK)).astype(
            jnp.bfloat16
        )


def shards(embed, values, match_frame, match_block, block_counts):
    frames = embed.shape[0]
    band_rows = embed.shape[1]
    half = embed.shape[2]
    blocks = band_rows // BLOCK
    hops = -(-REACH // frames)
    band_index = lax.axis_index("band")
    band_size = lax.axis_size("band")
    halo = 1 if band_size > 1 else 0
    chan_size = lax.axis_size("chan")
    chan_swap = [(i, (i + 1) % chan_size) for i in range(chan_size)]

    if halo:
        embed, rim_values = (with_halo(x, (("band", 1),), BLOCK) for x in (embed, values))
    else:
        rim_values = values
    rimmed_blocks = blocks + 2 * halo
    per_slab = frames * rimmed_blocks
    window_e = []
    window_v = []
    for offset in range(-hops, hops + 1):
        for own, window in ((embed, window_e), (rim_values, window_v)):
            slab = own if offset == 0 else passed_along(own, "frame", -offset)
            window.append(slab.reshape(per_slab, BLOCK, half))
    others = [lax.ppermute(slab, "chan", chan_swap) for slab in window_e]
    slabs = len(window_e)
    center = hops * per_slab

    frame_ids = jnp.arange(frames, dtype=jnp.int32)
    key_rows = (hops * frames + frame_ids[:, None, None] + match_frame) * rimmed_blocks
    key_cols = match_block - band_index * blocks + halo
    slot = jnp.clip(key_rows + key_cols, 0, slabs * per_slab - 1).astype(jnp.int32).reshape(-1)
    block_ids = band_index * blocks + jnp.arange(blocks, dtype=jnp.int32)
    active = (block_ids[None, :] < block_counts[:, None]).astype(jnp.int32)
    queries = frames * blocks

    kernel = functools.partial(
        aggregate_kernel,
        slabs=slabs,
        per_slab=per_slab,
        center=center,
        queries=queries,
        half=half,
        blocks=blocks,
        rimmed=rimmed_blocks,
        halo=halo,
    )
    smem = pl.BlockSpec(memory_space=pltpu.SMEM)
    hbm = pl.BlockSpec(memory_space=pl.ANY)
    vmem = pl.BlockSpec(memory_space=pltpu.VMEM)
    out_shape = [
        jax.ShapeDtypeStruct((per_slab, half, BLOCK), jnp.float32),
        jax.ShapeDtypeStruct((per_slab, 1, BLOCK), jnp.float32),
    ] + [
        jax.ShapeDtypeStruct((per_slab, half + MASS_ROWS, BLOCK), jnp.bfloat16)
        for _ in range(slabs - 1)
    ]
    total = slabs * per_slab
    outs = pl.pallas_call(
        kernel,
        out_shape=out_shape,
        in_specs=[smem, smem] + [vmem] * (3 * slabs),
        out_specs=[vmem] * len(out_shape),
        scratch_shapes=[
            pltpu.VMEM((total, BLOCK, 2 * half), jnp.bfloat16),
            pltpu.VMEM((total, BLOCK, half), jnp.bfloat16),
            pltpu.VMEM((total, half, BLOCK), jnp.float32),
            pltpu.VMEM((total, 1, BLOCK), jnp.float32),
            pltpu.VMEM((BLOCK, K * BLOCK), jnp.float32),
            pltpu.VMEM((K * BLOCK, half), jnp.bfloat16),
            pltpu.SemaphoreType.DMA((3, slabs)),
        ],
    )(slot, active.reshape(-1), *window_e, *others, *window_v)
    own_num, own_mass = outs[0], outs[1]
    remote = outs[2:]
    offsets = [o for o in range(-hops, hops + 1) if o != 0]
    for offset, outgoing in zip(offsets, remote):
        arrived = passed_along(outgoing, "frame", offset).astype(jnp.float32)
        own_num = own_num + arrived[:, :half, :]
        own_mass = own_mass + arrived[:, half : half + 1, :]
    own_num = own_num.reshape(frames, rimmed_blocks, half, BLOCK)
    own_mass = own_mass.reshape(frames, rimmed_blocks, BLOCK)
    if halo:
        for toward in (1, -1):
            rim_block = blocks + 1 if toward > 0 else 0
            target_block = 1 if toward > 0 else blocks
            arrived = (
                passed_along(own_num[:, rim_block].astype(jnp.bfloat16), "band", toward).astype(
                    jnp.float32
                ),
                passed_along(own_mass[:, rim_block].astype(jnp.bfloat16), "band", toward).astype(
                    jnp.float32
                ),
            )
            own_num = own_num.at[:, target_block].add(arrived[0])
            own_mass = own_mass.at[:, target_block].add(arrived[1])
        own_num = own_num[:, 1 : blocks + 1]
        own_mass = own_mass[:, 1 : blocks + 1]
    numer = jnp.swapaxes(own_num, -1, -2)
    value_blocks = values.reshape(frames, blocks, BLOCK, half).astype(jnp.float32)
    result = (numer + value_blocks) / (own_mass[..., None] + 1.0)
    return result.reshape(frames, band_rows, half).astype(jnp.bfloat16)


def solution(mesh):
    placed = (
        P(("reel", "frame"), "band", "chan"),
        P(("reel", "frame"), "band", "chan"),
        P(("reel", "frame"), "band", None),
        P(("reel", "frame"), "band", None),
        P(("reel", "frame")),
    )
    return jax.shard_map(
        shards,
        mesh=mesh,
        in_specs=placed,
        out_specs=P(("reel", "frame"), "band", "chan"),
        check_vma=False,
    )
```

```python
import functools
import math

import jax
import jax.numpy as jnp
from jax import lax
from jax.experimental import pallas as pl
from jax.experimental.pallas import tpu as pltpu
from jax.sharding import PartitionSpec as P

W = 256
BLOCK = 128
K = 16
REACH = 8
MASS_ROWS = 16


def with_halo(x, sides, width):
    for axis, dim in sides:
        size, length = (lax.axis_size(axis), x.shape[dim])
        up = [(i, (i + 1) % size) for i in range(size - 1)]
        down = [(j, i) for i, j in up]
        last = lax.slice_in_dim(x, length - width, length, axis=dim)
        initial = lax.slice_in_dim(x, 0, width, axis=dim)
        before = lax.ppermute(last, axis, up)
        after = lax.ppermute(initial, axis, down)
        x = jnp.concatenate([before, x, after], axis=dim)
    return x


def passed_along(block, axis, distance):
    devices = range(lax.axis_size(axis))
    route = [(i - distance, i) for i in devices if i - distance in devices]
    return lax.ppermute(block, axis, route)


def aggregate_kernel(
    slot_ref, act_ref, *refs, slabs, per_slab, center, queries, half, blocks, rimmed, halo
):
    sources = [refs[:slabs], refs[2 * slabs : 3 * slabs], refs[slabs : 2 * slabs]]
    own_num_ref, own_mass_ref = refs[3 * slabs : 3 * slabs + 2]
    remote_refs = refs[3 * slabs + 2 : 4 * slabs + 1]
    key_e, key_v, acc, macc, score_ref, value_ref, sems = refs[4 * slabs + 1 :]

    copies = []
    for s in range(slabs):
        dst = pl.ds(s * per_slab, per_slab)
        targets = (
            key_e.at[dst, :, pl.ds(0, half)],
            key_v.at[dst],
            key_e.at[dst, :, pl.ds(half, half)],
        )
        for kind, target in enumerate(targets):
            copies.append(pltpu.make_async_copy(sources[kind][s], target, sems.at[kind, s]))
    for c in copies:
        c.start()
    acc[...] = jnp.zeros(acc.shape, acc.dtype)
    macc[...] = jnp.zeros(macc.shape, macc.dtype)
    for c in copies:
        c.wait()

    score_scale = 1.0 / math.sqrt(W)
    dims_t = (((1,), (1,)), ((), ()))

    def one_query(i, carry):
        q_slot = center + (i // blocks) * rimmed + halo + i % blocks
        query = key_e[q_slot] * jnp.asarray(score_scale, jnp.bfloat16)
        slots = [slot_ref[i * K + k] for k in range(K)]
        for k in range(K):
            s = slots[k]
            part = lax.dot_general(query, key_e[s], dims_t, preferred_element_type=jnp.float32)
            score_ref[:, k * BLOCK : (k + 1) * BLOCK] = part
            value_ref[k * BLOCK : (k + 1) * BLOCK, :] = key_v[s]
        score = score_ref[...]
        peak = jnp.max(score, axis=-1, keepdims=True)
        exponent = jnp.exp(score - peak)
        prob = exponent / jnp.sum(exponent, axis=-1, keepdims=True)
        attention = prob.astype(jnp.bfloat16)
        estimate = jnp.dot(attention, value_ref[...], preferred_element_type=jnp.float32)
        active = act_ref[i].astype(jnp.float32)
        estimate = estimate.astype(jnp.bfloat16).astype(jnp.float32) * active
        estimate_t = estimate.T.astype(jnp.bfloat16)
        contrib_t = jnp.dot(estimate_t, attention, preferred_element_type=jnp.float32)
        weights = jnp.sum(prob, axis=0, keepdims=True) * active
        for k in range(K):
            s = slots[k]
            acc[s] = acc[s] + contrib_t[:, k * BLOCK : (k + 1) * BLOCK]
            macc[s] = macc[s] + weights[:, k * BLOCK : (k + 1) * BLOCK]
        return carry

    lax.fori_loop(0, queries, one_query, 0)

    own = pl.ds(center, per_slab)
    own_num_ref[...] = acc[own]
    own_mass_ref[...] = macc[own]
    remote = [s for s in range(slabs) if s * per_slab != center]
    mass_rows = -(-per_slab // MASS_ROWS) * MASS_ROWS
    for ref, s in zip(remote_refs, remote):
        rows = pl.ds(s * per_slab, per_slab)
        ref[: per_slab * half, :] = acc[rows].reshape(per_slab * half, BLOCK).astype(jnp.bfloat16)
        spread = [macc[s * per_slab + j] for j in range(per_slab)]
        if mass_rows > per_slab:
            spread.append(jnp.zeros((mass_rows - per_slab, BLOCK), jnp.float32))
        ref[per_slab * half :, :] = jnp.concatenate(spread, axis=0).astype(jnp.bfloat16)


def shards(embed, values, match_frame, match_block, block_counts):
    frames = embed.shape[0]
    band_rows = embed.shape[1]
    half = embed.shape[2]
    blocks = band_rows // BLOCK
    hops = -(-REACH // frames)
    band_index = lax.axis_index("band")
    band_size = lax.axis_size("band")
    halo = 1 if band_size > 1 else 0
    chan_size = lax.axis_size("chan")
    chan_swap = [(i, (i + 1) % chan_size) for i in range(chan_size)]

    if halo:
        embed, rim_values = (with_halo(x, (("band", 1),), BLOCK) for x in (embed, values))
    else:
        rim_values = values
    rimmed_blocks = blocks + 2 * halo
    per_slab = frames * rimmed_blocks
    window_e = []
    window_v = []
    for offset in range(-hops, hops + 1):
        for own, window in ((embed, window_e), (rim_values, window_v)):
            slab = own if offset == 0 else passed_along(own, "frame", -offset)
            window.append(slab.reshape(per_slab, BLOCK, half))
    others = [lax.ppermute(slab, "chan", chan_swap) for slab in window_e]
    slabs = len(window_e)
    center = hops * per_slab

    frame_ids = jnp.arange(frames, dtype=jnp.int32)
    key_rows = (hops * frames + frame_ids[:, None, None] + match_frame) * rimmed_blocks
    key_cols = match_block - band_index * blocks + halo
    slot = jnp.clip(key_rows + key_cols, 0, slabs * per_slab - 1).astype(jnp.int32).reshape(-1)
    block_ids = band_index * blocks + jnp.arange(blocks, dtype=jnp.int32)
    active = (block_ids[None, :] < block_counts[:, None]).astype(jnp.int32)
    queries = frames * blocks

    kernel = functools.partial(
        aggregate_kernel,
        slabs=slabs,
        per_slab=per_slab,
        center=center,
        queries=queries,
        half=half,
        blocks=blocks,
        rimmed=rimmed_blocks,
        halo=halo,
    )
    smem = pl.BlockSpec(memory_space=pltpu.SMEM)
    hbm = pl.BlockSpec(memory_space=pl.ANY)
    vmem = pl.BlockSpec(memory_space=pltpu.VMEM)
    mass_rows = -(-per_slab // MASS_ROWS) * MASS_ROWS
    out_shape = [
        jax.ShapeDtypeStruct((per_slab, half, BLOCK), jnp.float32),
        jax.ShapeDtypeStruct((per_slab, 1, BLOCK), jnp.float32),
    ] + [
        jax.ShapeDtypeStruct((per_slab * half + mass_rows, BLOCK), jnp.bfloat16)
        for _ in range(slabs - 1)
    ]
    total = slabs * per_slab
    outs = pl.pallas_call(
        kernel,
        out_shape=out_shape,
        in_specs=[smem, smem] + [vmem] * (3 * slabs),
        out_specs=[vmem] * len(out_shape),
        scratch_shapes=[
            pltpu.VMEM((total, BLOCK, 2 * half), jnp.bfloat16),
            pltpu.VMEM((total, BLOCK, half), jnp.bfloat16),
            pltpu.VMEM((total, half, BLOCK), jnp.float32),
            pltpu.VMEM((total, 1, BLOCK), jnp.float32),
            pltpu.VMEM((BLOCK, K * BLOCK), jnp.float32),
            pltpu.VMEM((K * BLOCK, half), jnp.bfloat16),
            pltpu.SemaphoreType.DMA((3, slabs)),
        ],
    )(slot, active.reshape(-1), *window_e, *others, *window_v)
    own_num, own_mass = outs[0], outs[1]
    remote = outs[2:]
    offsets = [o for o in range(-hops, hops + 1) if o != 0]
    for offset, outgoing in zip(offsets, remote):
        arrived = passed_along(outgoing, "frame", offset).astype(jnp.float32)
        own_num = own_num + arrived[: per_slab * half].reshape(per_slab, half, BLOCK)
        own_mass = own_mass + arrived[per_slab * half : per_slab * half + per_slab][:, None, :]
    own_num = own_num.reshape(frames, rimmed_blocks, half, BLOCK)
    own_mass = own_mass.reshape(frames, rimmed_blocks, BLOCK)
    if halo:
        for toward in (1, -1):
            rim_block = blocks + 1 if toward > 0 else 0
            target_block = 1 if toward > 0 else blocks
            arrived = (
                passed_along(own_num[:, rim_block].astype(jnp.bfloat16), "band", toward).astype(
                    jnp.float32
                ),
                passed_along(own_mass[:, rim_block].astype(jnp.bfloat16), "band", toward).astype(
                    jnp.float32
                ),
            )
            own_num = own_num.at[:, target_block].add(arrived[0])
            own_mass = own_mass.at[:, target_block].add(arrived[1])
        own_num = own_num[:, 1 : blocks + 1]
        own_mass = own_mass[:, 1 : blocks + 1]
    numer = jnp.swapaxes(own_num, -1, -2)
    value_blocks = values.reshape(frames, blocks, BLOCK, half).astype(jnp.float32)
    result = (numer + value_blocks) / (own_mass[..., None] + 1.0)
    return result.reshape(frames, band_rows, half).astype(jnp.bfloat16)


def solution(mesh):
    placed = (
        P(("reel", "frame"), "band", "chan"),
        P(("reel", "frame"), "band", "chan"),
        P(("reel", "frame"), "band", None),
        P(("reel", "frame"), "band", None),
        P(("reel", "frame")),
    )
    return jax.shard_map(
        shards,
        mesh=mesh,
        in_specs=placed,
        out_specs=P(("reel", "frame"), "band", "chan"),
        check_vma=False,
    )
```

```python
import functools
import math

import jax
import jax.numpy as jnp
from jax import lax
from jax.experimental import pallas as pl
from jax.experimental.pallas import tpu as pltpu
from jax.sharding import PartitionSpec as P

W = 256
BLOCK = 128
K = 16
REACH = 8
MASS_ROWS = 16


def with_halo(x, sides, width):
    for axis, dim in sides:
        size, length = (lax.axis_size(axis), x.shape[dim])
        up = [(i, (i + 1) % size) for i in range(size - 1)]
        down = [(j, i) for i, j in up]
        last = lax.slice_in_dim(x, length - width, length, axis=dim)
        initial = lax.slice_in_dim(x, 0, width, axis=dim)
        before = lax.ppermute(last, axis, up)
        after = lax.ppermute(initial, axis, down)
        x = jnp.concatenate([before, x, after], axis=dim)
    return x


def passed_along(block, axis, distance):
    devices = range(lax.axis_size(axis))
    route = [(i - distance, i) for i in devices if i - distance in devices]
    return lax.ppermute(block, axis, route)


def aggregate_kernel(
    slot_ref, act_ref, *refs, slabs, per_slab, center, queries, half, blocks, rimmed, halo
):
    sources = [refs[:slabs], refs[2 * slabs : 3 * slabs], refs[slabs : 2 * slabs]]
    own_num_ref, own_mass_ref = refs[3 * slabs : 3 * slabs + 2]
    remote_refs = refs[3 * slabs + 2 : 4 * slabs + 1]
    key_e, key_v, acc, macc, key_ref, value_ref, sems = refs[4 * slabs + 1 :]

    copies = []
    for s in range(slabs):
        dst = pl.ds(s * per_slab, per_slab)
        targets = (
            key_e.at[dst, :, pl.ds(0, half)],
            key_v.at[dst],
            key_e.at[dst, :, pl.ds(half, half)],
        )
        for kind, target in enumerate(targets):
            copies.append(pltpu.make_async_copy(sources[kind][s], target, sems.at[kind, s]))
    for c in copies:
        c.start()
    acc[...] = jnp.zeros(acc.shape, acc.dtype)
    macc[...] = jnp.zeros(macc.shape, macc.dtype)
    for c in copies:
        c.wait()

    score_scale = 1.0 / math.sqrt(W)
    dims_t = (((1,), (1,)), ((), ()))

    def one_query(i, carry):
        q_slot = center + (i // blocks) * rimmed + halo + i % blocks
        query = key_e[q_slot] * jnp.asarray(score_scale, jnp.bfloat16)
        slots = [slot_ref[i * K + k] for k in range(K)]
        for k in range(K):
            s = slots[k]
            key_ref[k * BLOCK : (k + 1) * BLOCK, :] = key_e[s]
            value_ref[k * BLOCK : (k + 1) * BLOCK, :] = key_v[s]
        score = lax.dot_general(query, key_ref[...], dims_t, preferred_element_type=jnp.float32)
        peak = jnp.max(score, axis=-1, keepdims=True)
        exponent = jnp.exp(score - peak)
        prob = exponent / jnp.sum(exponent, axis=-1, keepdims=True)
        attention = prob.astype(jnp.bfloat16)
        estimate = jnp.dot(attention, value_ref[...], preferred_element_type=jnp.float32)
        active = act_ref[i].astype(jnp.float32)
        estimate = estimate.astype(jnp.bfloat16).astype(jnp.float32) * active
        estimate_t = estimate.T.astype(jnp.bfloat16)
        contrib_t = jnp.dot(estimate_t, attention, preferred_element_type=jnp.float32)
        weights = jnp.sum(prob, axis=0, keepdims=True) * active
        for k in range(K):
            s = slots[k]
            acc[s] = acc[s] + contrib_t[:, k * BLOCK : (k + 1) * BLOCK]
            macc[s] = macc[s] + weights[:, k * BLOCK : (k + 1) * BLOCK]
        return carry

    lax.fori_loop(0, queries, one_query, 0)

    own = pl.ds(center, per_slab)
    own_num_ref[...] = acc[own]
    own_mass_ref[...] = macc[own]
    remote = [s for s in range(slabs) if s * per_slab != center]
    mass_rows = -(-per_slab // MASS_ROWS) * MASS_ROWS
    for ref, s in zip(remote_refs, remote):
        rows = pl.ds(s * per_slab, per_slab)
        ref[: per_slab * half, :] = acc[rows].reshape(per_slab * half, BLOCK).astype(jnp.bfloat16)
        spread = [macc[s * per_slab + j] for j in range(per_slab)]
        if mass_rows > per_slab:
            spread.append(jnp.zeros((mass_rows - per_slab, BLOCK), jnp.float32))
        ref[per_slab * half :, :] = jnp.concatenate(spread, axis=0).astype(jnp.bfloat16)


def shards(embed, values, match_frame, match_block, block_counts):
    frames = embed.shape[0]
    band_rows = embed.shape[1]
    half = embed.shape[2]
    blocks = band_rows // BLOCK
    hops = -(-REACH // frames)
    band_index = lax.axis_index("band")
    band_size = lax.axis_size("band")
    halo = 1 if band_size > 1 else 0
    chan_size = lax.axis_size("chan")
    chan_swap = [(i, (i + 1) % chan_size) for i in range(chan_size)]

    if halo:
        embed, rim_values = (with_halo(x, (("band", 1),), BLOCK) for x in (embed, values))
    else:
        rim_values = values
    rimmed_blocks = blocks + 2 * halo
    per_slab = frames * rimmed_blocks
    window_e = []
    window_v = []
    for offset in range(-hops, hops + 1):
        for own, window in ((embed, window_e), (rim_values, window_v)):
            slab = own if offset == 0 else passed_along(own, "frame", -offset)
            window.append(slab.reshape(per_slab, BLOCK, half))
    others = [lax.ppermute(slab, "chan", chan_swap) for slab in window_e]
    slabs = len(window_e)
    center = hops * per_slab

    frame_ids = jnp.arange(frames, dtype=jnp.int32)
    key_rows = (hops * frames + frame_ids[:, None, None] + match_frame) * rimmed_blocks
    key_cols = match_block - band_index * blocks + halo
    slot = jnp.clip(key_rows + key_cols, 0, slabs * per_slab - 1).astype(jnp.int32).reshape(-1)
    block_ids = band_index * blocks + jnp.arange(blocks, dtype=jnp.int32)
    active = (block_ids[None, :] < block_counts[:, None]).astype(jnp.int32)
    queries = frames * blocks

    kernel = functools.partial(
        aggregate_kernel,
        slabs=slabs,
        per_slab=per_slab,
        center=center,
        queries=queries,
        half=half,
        blocks=blocks,
        rimmed=rimmed_blocks,
        halo=halo,
    )
    smem = pl.BlockSpec(memory_space=pltpu.SMEM)
    hbm = pl.BlockSpec(memory_space=pl.ANY)
    vmem = pl.BlockSpec(memory_space=pltpu.VMEM)
    mass_rows = -(-per_slab // MASS_ROWS) * MASS_ROWS
    out_shape = [
        jax.ShapeDtypeStruct((per_slab, half, BLOCK), jnp.float32),
        jax.ShapeDtypeStruct((per_slab, 1, BLOCK), jnp.float32),
    ] + [
        jax.ShapeDtypeStruct((per_slab * half + mass_rows, BLOCK), jnp.bfloat16)
        for _ in range(slabs - 1)
    ]
    total = slabs * per_slab
    outs = pl.pallas_call(
        kernel,
        out_shape=out_shape,
        in_specs=[smem, smem] + [vmem] * (3 * slabs),
        out_specs=[vmem] * len(out_shape),
        scratch_shapes=[
            pltpu.VMEM((total, BLOCK, 2 * half), jnp.bfloat16),
            pltpu.VMEM((total, BLOCK, half), jnp.bfloat16),
            pltpu.VMEM((total, half, BLOCK), jnp.float32),
            pltpu.VMEM((total, 1, BLOCK), jnp.float32),
            pltpu.VMEM((K * BLOCK, 2 * half), jnp.bfloat16),
            pltpu.VMEM((K * BLOCK, half), jnp.bfloat16),
            pltpu.SemaphoreType.DMA((3, slabs)),
        ],
    )(slot, active.reshape(-1), *window_e, *others, *window_v)
    own_num, own_mass = outs[0], outs[1]
    remote = outs[2:]
    offsets = [o for o in range(-hops, hops + 1) if o != 0]
    for offset, outgoing in zip(offsets, remote):
        arrived = passed_along(outgoing, "frame", offset).astype(jnp.float32)
        own_num = own_num + arrived[: per_slab * half].reshape(per_slab, half, BLOCK)
        own_mass = own_mass + arrived[per_slab * half : per_slab * half + per_slab][:, None, :]
    own_num = own_num.reshape(frames, rimmed_blocks, half, BLOCK)
    own_mass = own_mass.reshape(frames, rimmed_blocks, BLOCK)
    if halo:
        for toward in (1, -1):
            rim_block = blocks + 1 if toward > 0 else 0
            target_block = 1 if toward > 0 else blocks
            arrived = (
                passed_along(own_num[:, rim_block].astype(jnp.bfloat16), "band", toward).astype(
                    jnp.float32
                ),
                passed_along(own_mass[:, rim_block].astype(jnp.bfloat16), "band", toward).astype(
                    jnp.float32
                ),
            )
            own_num = own_num.at[:, target_block].add(arrived[0])
            own_mass = own_mass.at[:, target_block].add(arrived[1])
        own_num = own_num[:, 1 : blocks + 1]
        own_mass = own_mass[:, 1 : blocks + 1]
    numer = jnp.swapaxes(own_num, -1, -2)
    value_blocks = values.reshape(frames, blocks, BLOCK, half).astype(jnp.float32)
    result = (numer + value_blocks) / (own_mass[..., None] + 1.0)
    return result.reshape(frames, band_rows, half).astype(jnp.bfloat16)


def solution(mesh):
    placed = (
        P(("reel", "frame"), "band", "chan"),
        P(("reel", "frame"), "band", "chan"),
        P(("reel", "frame"), "band", None),
        P(("reel", "frame"), "band", None),
        P(("reel", "frame")),
    )
    return jax.shard_map(
        shards,
        mesh=mesh,
        in_specs=placed,
        out_specs=P(("reel", "frame"), "band", "chan"),
        check_vma=False,
    )
```

```python
import functools
import math

import jax
import jax.numpy as jnp
from jax import lax
from jax.experimental import pallas as pl
from jax.experimental.pallas import tpu as pltpu
from jax.sharding import PartitionSpec as P

W = 256
BLOCK = 128
K = 16
REACH = 8
MASS_ROWS = 16


def with_halo(x, sides, width):
    for axis, dim in sides:
        size, length = (lax.axis_size(axis), x.shape[dim])
        up = [(i, (i + 1) % size) for i in range(size - 1)]
        down = [(j, i) for i, j in up]
        last = lax.slice_in_dim(x, length - width, length, axis=dim)
        initial = lax.slice_in_dim(x, 0, width, axis=dim)
        before = lax.ppermute(last, axis, up)
        after = lax.ppermute(initial, axis, down)
        x = jnp.concatenate([before, x, after], axis=dim)
    return x


def passed_along(block, axis, distance):
    devices = range(lax.axis_size(axis))
    route = [(i - distance, i) for i in devices if i - distance in devices]
    return lax.ppermute(block, axis, route)


def aggregate_kernel(
    slot_ref, act_ref, *refs, slabs, per_slab, center, queries, half, blocks, rimmed, halo
):
    mine_refs, other_refs, value_refs = refs[:slabs], refs[slabs : 2 * slabs], refs[2 * slabs : 3 * slabs]
    own_num_ref, own_mass_ref = refs[3 * slabs : 3 * slabs + 2]
    remote_refs = refs[3 * slabs + 2 : 4 * slabs + 1]
    acc, macc, query_ref, key_ref, value_ref = refs[4 * slabs + 1 :]

    acc[...] = jnp.zeros(acc.shape, acc.dtype)
    macc[...] = jnp.zeros(macc.shape, macc.dtype)

    score_scale = 1.0 / math.sqrt(W)
    dims_t = (((1,), (1,)), ((), ()))
    middle = center // per_slab

    def one_query(i, carry):
        q_local = (i // blocks) * rimmed + halo + i % blocks
        query_ref[:, :half] = mine_refs[middle][q_local]
        query_ref[:, half:] = other_refs[middle][q_local]
        query = query_ref[...] * jnp.asarray(score_scale, jnp.bfloat16)
        slots = [slot_ref[i * K + k] for k in range(K)]
        for k in range(K):
            slab = slots[k] // per_slab
            local = slots[k] % per_slab
            rows = pl.ds(k * BLOCK, BLOCK)
            for j in range(slabs):

                @pl.when(slab == j)
                def _():
                    key_ref[rows, :half] = mine_refs[j][local]
                    key_ref[rows, half:] = other_refs[j][local]
                    value_ref[rows, :] = value_refs[j][local]

        score = lax.dot_general(query, key_ref[...], dims_t, preferred_element_type=jnp.float32)
        peak = jnp.max(score, axis=-1, keepdims=True)
        exponent = jnp.exp(score - peak)
        prob = exponent / jnp.sum(exponent, axis=-1, keepdims=True)
        attention = prob.astype(jnp.bfloat16)
        estimate = jnp.dot(attention, value_ref[...], preferred_element_type=jnp.float32)
        active = act_ref[i].astype(jnp.float32)
        estimate = estimate.astype(jnp.bfloat16).astype(jnp.float32) * active
        estimate_t = estimate.T.astype(jnp.bfloat16)
        contrib_t = jnp.dot(estimate_t, attention, preferred_element_type=jnp.float32)
        weights = jnp.sum(prob, axis=0, keepdims=True) * active
        for k in range(K):
            s = slots[k]
            acc[s] = acc[s] + contrib_t[:, k * BLOCK : (k + 1) * BLOCK]
            macc[s] = macc[s] + weights[:, k * BLOCK : (k + 1) * BLOCK]
        return carry

    lax.fori_loop(0, queries, one_query, 0)

    own = pl.ds(center, per_slab)
    own_num_ref[...] = acc[own]
    own_mass_ref[...] = macc[own]
    remote = [s for s in range(slabs) if s * per_slab != center]
    mass_rows = -(-per_slab // MASS_ROWS) * MASS_ROWS
    for ref, s in zip(remote_refs, remote):
        rows = pl.ds(s * per_slab, per_slab)
        ref[: per_slab * half, :] = acc[rows].reshape(per_slab * half, BLOCK).astype(jnp.bfloat16)
        spread = [macc[s * per_slab + j] for j in range(per_slab)]
        if mass_rows > per_slab:
            spread.append(jnp.zeros((mass_rows - per_slab, BLOCK), jnp.float32))
        ref[per_slab * half :, :] = jnp.concatenate(spread, axis=0).astype(jnp.bfloat16)


def shards(embed, values, match_frame, match_block, block_counts):
    frames = embed.shape[0]
    band_rows = embed.shape[1]
    half = embed.shape[2]
    blocks = band_rows // BLOCK
    hops = -(-REACH // frames)
    band_index = lax.axis_index("band")
    band_size = lax.axis_size("band")
    halo = 1 if band_size > 1 else 0
    chan_size = lax.axis_size("chan")
    chan_swap = [(i, (i + 1) % chan_size) for i in range(chan_size)]

    if halo:
        embed, rim_values = (with_halo(x, (("band", 1),), BLOCK) for x in (embed, values))
    else:
        rim_values = values
    rimmed_blocks = blocks + 2 * halo
    per_slab = frames * rimmed_blocks
    window_e = []
    window_v = []
    for offset in range(-hops, hops + 1):
        for own, window in ((embed, window_e), (rim_values, window_v)):
            slab = own if offset == 0 else passed_along(own, "frame", -offset)
            window.append(slab.reshape(per_slab, BLOCK, half))
    others = [lax.ppermute(slab, "chan", chan_swap) for slab in window_e]
    slabs = len(window_e)
    center = hops * per_slab

    frame_ids = jnp.arange(frames, dtype=jnp.int32)
    key_rows = (hops * frames + frame_ids[:, None, None] + match_frame) * rimmed_blocks
    key_cols = match_block - band_index * blocks + halo
    slot = jnp.clip(key_rows + key_cols, 0, slabs * per_slab - 1).astype(jnp.int32).reshape(-1)
    block_ids = band_index * blocks + jnp.arange(blocks, dtype=jnp.int32)
    active = (block_ids[None, :] < block_counts[:, None]).astype(jnp.int32)
    queries = frames * blocks

    kernel = functools.partial(
        aggregate_kernel,
        slabs=slabs,
        per_slab=per_slab,
        center=center,
        queries=queries,
        half=half,
        blocks=blocks,
        rimmed=rimmed_blocks,
        halo=halo,
    )
    smem = pl.BlockSpec(memory_space=pltpu.SMEM)
    hbm = pl.BlockSpec(memory_space=pl.ANY)
    vmem = pl.BlockSpec(memory_space=pltpu.VMEM)
    mass_rows = -(-per_slab // MASS_ROWS) * MASS_ROWS
    out_shape = [
        jax.ShapeDtypeStruct((per_slab, half, BLOCK), jnp.float32),
        jax.ShapeDtypeStruct((per_slab, 1, BLOCK), jnp.float32),
    ] + [
        jax.ShapeDtypeStruct((per_slab * half + mass_rows, BLOCK), jnp.bfloat16)
        for _ in range(slabs - 1)
    ]
    total = slabs * per_slab
    outs = pl.pallas_call(
        kernel,
        out_shape=out_shape,
        in_specs=[smem, smem] + [vmem] * (3 * slabs),
        out_specs=[vmem] * len(out_shape),
        scratch_shapes=[
            pltpu.VMEM((total, half, BLOCK), jnp.float32),
            pltpu.VMEM((total, 1, BLOCK), jnp.float32),
            pltpu.VMEM((BLOCK, 2 * half), jnp.bfloat16),
            pltpu.VMEM((K * BLOCK, 2 * half), jnp.bfloat16),
            pltpu.VMEM((K * BLOCK, half), jnp.bfloat16),
        ],
    )(slot, active.reshape(-1), *window_e, *others, *window_v)
    own_num, own_mass = outs[0], outs[1]
    remote = outs[2:]
    offsets = [o for o in range(-hops, hops + 1) if o != 0]
    for offset, outgoing in zip(offsets, remote):
        arrived = passed_along(outgoing, "frame", offset).astype(jnp.float32)
        own_num = own_num + arrived[: per_slab * half].reshape(per_slab, half, BLOCK)
        own_mass = own_mass + arrived[per_slab * half : per_slab * half + per_slab][:, None, :]
    own_num = own_num.reshape(frames, rimmed_blocks, half, BLOCK)
    own_mass = own_mass.reshape(frames, rimmed_blocks, BLOCK)
    if halo:
        for toward in (1, -1):
            rim_block = blocks + 1 if toward > 0 else 0
            target_block = 1 if toward > 0 else blocks
            arrived = (
                passed_along(own_num[:, rim_block].astype(jnp.bfloat16), "band", toward).astype(
                    jnp.float32
                ),
                passed_along(own_mass[:, rim_block].astype(jnp.bfloat16), "band", toward).astype(
                    jnp.float32
                ),
            )
            own_num = own_num.at[:, target_block].add(arrived[0])
            own_mass = own_mass.at[:, target_block].add(arrived[1])
        own_num = own_num[:, 1 : blocks + 1]
        own_mass = own_mass[:, 1 : blocks + 1]
    numer = jnp.swapaxes(own_num, -1, -2)
    value_blocks = values.reshape(frames, blocks, BLOCK, half).astype(jnp.float32)
    result = (numer + value_blocks) / (own_mass[..., None] + 1.0)
    return result.reshape(frames, band_rows, half).astype(jnp.bfloat16)


def solution(mesh):
    placed = (
        P(("reel", "frame"), "band", "chan"),
        P(("reel", "frame"), "band", "chan"),
        P(("reel", "frame"), "band", None),
        P(("reel", "frame"), "band", None),
        P(("reel", "frame")),
    )
    return jax.shard_map(
        shards,
        mesh=mesh,
        in_specs=placed,
        out_specs=P(("reel", "frame"), "band", "chan"),
        check_vma=False,
    )
```

```python
import functools
import math

import jax
import jax.numpy as jnp
from jax import lax
from jax.experimental import pallas as pl
from jax.experimental.pallas import tpu as pltpu
from jax.sharding import PartitionSpec as P

W = 256
BLOCK = 128
K = 16
REACH = 8
MASS_ROWS = 16


def with_halo(x, sides, width):
    for axis, dim in sides:
        size, length = (lax.axis_size(axis), x.shape[dim])
        up = [(i, (i + 1) % size) for i in range(size - 1)]
        down = [(j, i) for i, j in up]
        last = lax.slice_in_dim(x, length - width, length, axis=dim)
        initial = lax.slice_in_dim(x, 0, width, axis=dim)
        before = lax.ppermute(last, axis, up)
        after = lax.ppermute(initial, axis, down)
        x = jnp.concatenate([before, x, after], axis=dim)
    return x


def passed_along(block, axis, distance):
    devices = range(lax.axis_size(axis))
    route = [(i - distance, i) for i in devices if i - distance in devices]
    return lax.ppermute(block, axis, route)


def aggregate_kernel(
    slot_ref, act_ref, *refs, slabs, per_slab, center, queries, half, blocks, rimmed, halo
):
    sources = [refs[:slabs], refs[2 * slabs : 3 * slabs], refs[slabs : 2 * slabs]]
    own_num_ref, own_mass_ref = refs[3 * slabs : 3 * slabs + 2]
    remote_refs = refs[3 * slabs + 2 : 4 * slabs + 1]
    key_e, key_v, acc, macc, score_ref, value_ref, sems = refs[4 * slabs + 1 :]

    copies = []
    for s in range(slabs):
        dst = pl.ds(s * per_slab, per_slab)
        targets = (
            key_e.at[dst, :, pl.ds(0, half)],
            key_v.at[dst],
            key_e.at[dst, :, pl.ds(half, half)],
        )
        for kind, target in enumerate(targets):
            copies.append(pltpu.make_async_copy(sources[kind][s], target, sems.at[kind, s]))
    for c in copies:
        c.start()
    acc[...] = jnp.zeros(acc.shape, acc.dtype)
    macc[...] = jnp.zeros(macc.shape, macc.dtype)
    for c in copies:
        c.wait()

    score_scale = 1.0 / math.sqrt(W)
    dims_t = (((1,), (1,)), ((), ()))

    def one_query(i, carry):
        q_slot = center + (i // blocks) * rimmed + halo + i % blocks
        query = key_e[q_slot] * jnp.asarray(score_scale, jnp.bfloat16)
        slots = [slot_ref[i * K + k] for k in range(K)]
        for k in range(K):
            s = slots[k]
            part = lax.dot_general(query, key_e[s], dims_t, preferred_element_type=jnp.float32)
            score_ref[:, k * BLOCK : (k + 1) * BLOCK] = part
            value_ref[k * BLOCK : (k + 1) * BLOCK, :] = key_v[s]
        score = score_ref[...]
        peak = jnp.max(score, axis=-1, keepdims=True)
        exponent = jnp.exp(score - peak)
        prob = exponent / jnp.sum(exponent, axis=-1, keepdims=True)
        attention = prob.astype(jnp.bfloat16)
        estimate = jnp.dot(attention, value_ref[...], preferred_element_type=jnp.float32)
        active = act_ref[i].astype(jnp.float32)
        estimate = estimate.astype(jnp.bfloat16).astype(jnp.float32) * active
        estimate_t = estimate.T.astype(jnp.bfloat16)
        contrib_t = jnp.dot(estimate_t, attention, preferred_element_type=jnp.float32)
        weights = jnp.sum(prob, axis=0, keepdims=True) * active
        for k in range(K):
            s = slots[k]
            acc[s] = acc[s] + contrib_t[:, k * BLOCK : (k + 1) * BLOCK]
            macc[s] = macc[s] + weights[:, k * BLOCK : (k + 1) * BLOCK]
        return carry

    lax.fori_loop(0, queries, one_query, 0)

    own = pl.ds(center, per_slab)
    own_num_ref[...] = acc[own]
    own_mass_ref[...] = macc[own]
    remote = [s for s in range(slabs) if s * per_slab != center]
    mass_rows = -(-per_slab // MASS_ROWS) * MASS_ROWS
    for ref, s in zip(remote_refs, remote):
        rows = pl.ds(s * per_slab, per_slab)
        ref[: per_slab * half, :] = acc[rows].reshape(per_slab * half, BLOCK).astype(jnp.bfloat16)
        spread = [macc[s * per_slab + j] for j in range(per_slab)]
        if mass_rows > per_slab:
            spread.append(jnp.zeros((mass_rows - per_slab, BLOCK), jnp.float32))
        ref[per_slab * half :, :] = jnp.concatenate(spread, axis=0).astype(jnp.bfloat16)


def combine_kernel(num_ref, mass_ref, values_ref, *refs, per_slab, half):
    arrived_refs = refs[:-1]
    out_ref = refs[-1]
    tail = per_slab * half
    masses = [ref[tail:, :].astype(jnp.float32) for ref in arrived_refs]
    for j in range(per_slab):
        numer = num_ref[j]
        mass = mass_ref[j]
        for ref, rows in zip(arrived_refs, masses):
            numer = numer + ref[j * half : (j + 1) * half, :].astype(jnp.float32)
            mass = mass + rows[j : j + 1]
        own = values_ref[j].astype(jnp.float32).T
        result = (numer + own) / (mass + 1.0)
        out_ref[j] = result.T.astype(jnp.bfloat16)


def shards(embed, values, match_frame, match_block, block_counts):
    frames = embed.shape[0]
    band_rows = embed.shape[1]
    half = embed.shape[2]
    blocks = band_rows // BLOCK
    hops = -(-REACH // frames)
    band_index = lax.axis_index("band")
    band_size = lax.axis_size("band")
    halo = 1 if band_size > 1 else 0
    chan_size = lax.axis_size("chan")
    chan_swap = [(i, (i + 1) % chan_size) for i in range(chan_size)]

    if halo:
        embed, rim_values = (with_halo(x, (("band", 1),), BLOCK) for x in (embed, values))
    else:
        rim_values = values
    rimmed_blocks = blocks + 2 * halo
    per_slab = frames * rimmed_blocks
    window_e = []
    window_v = []
    for offset in range(-hops, hops + 1):
        for own, window in ((embed, window_e), (rim_values, window_v)):
            slab = own if offset == 0 else passed_along(own, "frame", -offset)
            window.append(slab.reshape(per_slab, BLOCK, half))
    others = [lax.ppermute(slab, "chan", chan_swap) for slab in window_e]
    slabs = len(window_e)
    center = hops * per_slab

    frame_ids = jnp.arange(frames, dtype=jnp.int32)
    key_rows = (hops * frames + frame_ids[:, None, None] + match_frame) * rimmed_blocks
    key_cols = match_block - band_index * blocks + halo
    slot = jnp.clip(key_rows + key_cols, 0, slabs * per_slab - 1).astype(jnp.int32).reshape(-1)
    block_ids = band_index * blocks + jnp.arange(blocks, dtype=jnp.int32)
    active = (block_ids[None, :] < block_counts[:, None]).astype(jnp.int32)
    queries = frames * blocks

    kernel = functools.partial(
        aggregate_kernel,
        slabs=slabs,
        per_slab=per_slab,
        center=center,
        queries=queries,
        half=half,
        blocks=blocks,
        rimmed=rimmed_blocks,
        halo=halo,
    )
    smem = pl.BlockSpec(memory_space=pltpu.SMEM)
    hbm = pl.BlockSpec(memory_space=pl.ANY)
    vmem = pl.BlockSpec(memory_space=pltpu.VMEM)
    mass_rows = -(-per_slab // MASS_ROWS) * MASS_ROWS
    out_shape = [
        jax.ShapeDtypeStruct((per_slab, half, BLOCK), jnp.float32),
        jax.ShapeDtypeStruct((per_slab, 1, BLOCK), jnp.float32),
    ] + [
        jax.ShapeDtypeStruct((per_slab * half + mass_rows, BLOCK), jnp.bfloat16)
        for _ in range(slabs - 1)
    ]
    total = slabs * per_slab
    outs = pl.pallas_call(
        kernel,
        out_shape=out_shape,
        in_specs=[smem, smem] + [vmem] * (3 * slabs),
        out_specs=[vmem] * len(out_shape),
        scratch_shapes=[
            pltpu.VMEM((total, BLOCK, 2 * half), jnp.bfloat16),
            pltpu.VMEM((total, BLOCK, half), jnp.bfloat16),
            pltpu.VMEM((total, half, BLOCK), jnp.float32),
            pltpu.VMEM((total, 1, BLOCK), jnp.float32),
            pltpu.VMEM((BLOCK, K * BLOCK), jnp.float32),
            pltpu.VMEM((K * BLOCK, half), jnp.bfloat16),
            pltpu.SemaphoreType.DMA((3, slabs)),
        ],
    )(slot, active.reshape(-1), *window_e, *others, *window_v)
    own_num, own_mass = outs[0], outs[1]
    remote = outs[2:]
    offsets = [o for o in range(-hops, hops + 1) if o != 0]
    if not halo:
        arrivals = [passed_along(outgoing, "frame", offset) for offset, outgoing in zip(offsets, remote)]
        result = pl.pallas_call(
            functools.partial(combine_kernel, per_slab=per_slab, half=half),
            out_shape=jax.ShapeDtypeStruct((per_slab, BLOCK, half), jnp.bfloat16),
            in_specs=[vmem] * (3 + len(arrivals)),
            out_specs=vmem,
        )(own_num, own_mass, values.reshape(per_slab, BLOCK, half), *arrivals)
        return result.reshape(frames, band_rows, half)
    for offset, outgoing in zip(offsets, remote):
        arrived = passed_along(outgoing, "frame", offset).astype(jnp.float32)
        own_num = own_num + arrived[: per_slab * half].reshape(per_slab, half, BLOCK)
        own_mass = own_mass + arrived[per_slab * half : per_slab * half + per_slab][:, None, :]
    own_num = own_num.reshape(frames, rimmed_blocks, half, BLOCK)
    own_mass = own_mass.reshape(frames, rimmed_blocks, BLOCK)
    if halo:
        for toward in (1, -1):
            rim_block = blocks + 1 if toward > 0 else 0
            target_block = 1 if toward > 0 else blocks
            arrived = (
                passed_along(own_num[:, rim_block].astype(jnp.bfloat16), "band", toward).astype(
                    jnp.float32
                ),
                passed_along(own_mass[:, rim_block].astype(jnp.bfloat16), "band", toward).astype(
                    jnp.float32
                ),
            )
            own_num = own_num.at[:, target_block].add(arrived[0])
            own_mass = own_mass.at[:, target_block].add(arrived[1])
        own_num = own_num[:, 1 : blocks + 1]
        own_mass = own_mass[:, 1 : blocks + 1]
    numer = jnp.swapaxes(own_num, -1, -2)
    value_blocks = values.reshape(frames, blocks, BLOCK, half).astype(jnp.float32)
    result = (numer + value_blocks) / (own_mass[..., None] + 1.0)
    return result.reshape(frames, band_rows, half).astype(jnp.bfloat16)


def solution(mesh):
    placed = (
        P(("reel", "frame"), "band", "chan"),
        P(("reel", "frame"), "band", "chan"),
        P(("reel", "frame"), "band", None),
        P(("reel", "frame"), "band", None),
        P(("reel", "frame")),
    )
    return jax.shard_map(
        shards,
        mesh=mesh,
        in_specs=placed,
        out_specs=P(("reel", "frame"), "band", "chan"),
        check_vma=False,
    )
```

```python
import functools
import math

import jax
import jax.numpy as jnp
from jax import lax
from jax.experimental import pallas as pl
from jax.experimental.pallas import tpu as pltpu
from jax.sharding import PartitionSpec as P

W = 256
BLOCK = 128
K = 16
REACH = 8
MASS_ROWS = 16


def with_halo(x, sides, width):
    for axis, dim in sides:
        size, length = (lax.axis_size(axis), x.shape[dim])
        up = [(i, (i + 1) % size) for i in range(size - 1)]
        down = [(j, i) for i, j in up]
        last = lax.slice_in_dim(x, length - width, length, axis=dim)
        initial = lax.slice_in_dim(x, 0, width, axis=dim)
        before = lax.ppermute(last, axis, up)
        after = lax.ppermute(initial, axis, down)
        x = jnp.concatenate([before, x, after], axis=dim)
    return x


def passed_along(block, axis, distance):
    devices = range(lax.axis_size(axis))
    route = [(i - distance, i) for i in devices if i - distance in devices]
    return lax.ppermute(block, axis, route)


def aggregate_kernel(
    slot_ref, act_ref, *refs, slabs, per_slab, center, queries, half, blocks, rimmed, halo
):
    sources = [refs[:slabs], refs[2 * slabs : 3 * slabs], refs[slabs : 2 * slabs]]
    own_num_ref, own_mass_ref = refs[3 * slabs : 3 * slabs + 2]
    remote_refs = refs[3 * slabs + 2 : 4 * slabs + 1]
    key_e, key_v, acc, macc, score_ref, value_ref, sems = refs[4 * slabs + 1 :]

    copies = []
    for s in range(slabs):
        dst = pl.ds(s * per_slab, per_slab)
        targets = (
            key_e.at[dst, :, pl.ds(0, half)],
            key_v.at[dst],
            key_e.at[dst, :, pl.ds(half, half)],
        )
        for kind, target in enumerate(targets):
            copies.append(pltpu.make_async_copy(sources[kind][s], target, sems.at[kind, s]))
    for c in copies:
        c.start()
    acc[...] = jnp.zeros(acc.shape, acc.dtype)
    macc[...] = jnp.zeros(macc.shape, macc.dtype)
    for c in copies:
        c.wait()

    score_scale = 1.0 / math.sqrt(W)
    dims_t = (((1,), (1,)), ((), ()))

    def one_query(i, buf):
        q_slot = center + (i // blocks) * rimmed + halo + i % blocks
        query = key_e[q_slot] * jnp.asarray(score_scale, jnp.bfloat16)
        slots = [slot_ref[i * K + k] for k in range(K)]
        for k in range(K):
            s = slots[k]
            part = lax.dot_general(query, key_e[s], dims_t, preferred_element_type=jnp.float32)
            score_ref[buf, :, k * BLOCK : (k + 1) * BLOCK] = part
            value_ref[buf, k * BLOCK : (k + 1) * BLOCK, :] = key_v[s]
        score = score_ref[buf]
        peak = jnp.max(score, axis=-1, keepdims=True)
        exponent = jnp.exp(score - peak)
        prob = exponent / jnp.sum(exponent, axis=-1, keepdims=True)
        attention = prob.astype(jnp.bfloat16)
        estimate = jnp.dot(attention, value_ref[buf], preferred_element_type=jnp.float32)
        active = act_ref[i].astype(jnp.float32)
        estimate = estimate.astype(jnp.bfloat16).astype(jnp.float32) * active
        estimate_t = estimate.T.astype(jnp.bfloat16)
        contrib_t = jnp.dot(estimate_t, attention, preferred_element_type=jnp.float32)
        weights = jnp.sum(prob, axis=0, keepdims=True) * active
        for k in range(K):
            s = slots[k]
            acc[s] = acc[s] + contrib_t[:, k * BLOCK : (k + 1) * BLOCK]
            macc[s] = macc[s] + weights[:, k * BLOCK : (k + 1) * BLOCK]

    def query_pair(p, carry):
        one_query(2 * p, 0)
        one_query(2 * p + 1, 1)
        return carry

    lax.fori_loop(0, queries // 2, query_pair, 0)
    if queries % 2:
        one_query(queries - 1, 0)

    own = pl.ds(center, per_slab)
    own_num_ref[...] = acc[own]
    own_mass_ref[...] = macc[own]
    remote = [s for s in range(slabs) if s * per_slab != center]
    mass_rows = -(-per_slab // MASS_ROWS) * MASS_ROWS
    for ref, s in zip(remote_refs, remote):
        rows = pl.ds(s * per_slab, per_slab)
        ref[: per_slab * half, :] = acc[rows].reshape(per_slab * half, BLOCK).astype(jnp.bfloat16)
        spread = [macc[s * per_slab + j] for j in range(per_slab)]
        if mass_rows > per_slab:
            spread.append(jnp.zeros((mass_rows - per_slab, BLOCK), jnp.float32))
        ref[per_slab * half :, :] = jnp.concatenate(spread, axis=0).astype(jnp.bfloat16)


def combine_kernel(num_ref, mass_ref, values_ref, *refs, per_slab, half):
    arrived_refs = refs[:-1]
    out_ref = refs[-1]
    tail = per_slab * half
    masses = [ref[tail:, :].astype(jnp.float32) for ref in arrived_refs]
    for j in range(per_slab):
        numer = num_ref[j]
        mass = mass_ref[j]
        for ref, rows in zip(arrived_refs, masses):
            numer = numer + ref[j * half : (j + 1) * half, :].astype(jnp.float32)
            mass = mass + rows[j : j + 1]
        own = values_ref[j].astype(jnp.float32).T
        result = (numer + own) / (mass + 1.0)
        out_ref[j] = result.T.astype(jnp.bfloat16)


def shards(embed, values, match_frame, match_block, block_counts):
    frames = embed.shape[0]
    band_rows = embed.shape[1]
    half = embed.shape[2]
    blocks = band_rows // BLOCK
    hops = -(-REACH // frames)
    band_index = lax.axis_index("band")
    band_size = lax.axis_size("band")
    halo = 1 if band_size > 1 else 0
    chan_size = lax.axis_size("chan")
    chan_swap = [(i, (i + 1) % chan_size) for i in range(chan_size)]

    if halo:
        embed, rim_values = (with_halo(x, (("band", 1),), BLOCK) for x in (embed, values))
    else:
        rim_values = values
    rimmed_blocks = blocks + 2 * halo
    per_slab = frames * rimmed_blocks
    window_e = []
    window_v = []
    for offset in range(-hops, hops + 1):
        for own, window in ((embed, window_e), (rim_values, window_v)):
            slab = own if offset == 0 else passed_along(own, "frame", -offset)
            window.append(slab.reshape(per_slab, BLOCK, half))
    others = [lax.ppermute(slab, "chan", chan_swap) for slab in window_e]
    slabs = len(window_e)
    center = hops * per_slab

    frame_ids = jnp.arange(frames, dtype=jnp.int32)
    key_rows = (hops * frames + frame_ids[:, None, None] + match_frame) * rimmed_blocks
    key_cols = match_block - band_index * blocks + halo
    slot = jnp.clip(key_rows + key_cols, 0, slabs * per_slab - 1).astype(jnp.int32).reshape(-1)
    block_ids = band_index * blocks + jnp.arange(blocks, dtype=jnp.int32)
    active = (block_ids[None, :] < block_counts[:, None]).astype(jnp.int32)
    queries = frames * blocks

    kernel = functools.partial(
        aggregate_kernel,
        slabs=slabs,
        per_slab=per_slab,
        center=center,
        queries=queries,
        half=half,
        blocks=blocks,
        rimmed=rimmed_blocks,
        halo=halo,
    )
    smem = pl.BlockSpec(memory_space=pltpu.SMEM)
    hbm = pl.BlockSpec(memory_space=pl.ANY)
    vmem = pl.BlockSpec(memory_space=pltpu.VMEM)
    mass_rows = -(-per_slab // MASS_ROWS) * MASS_ROWS
    out_shape = [
        jax.ShapeDtypeStruct((per_slab, half, BLOCK), jnp.float32),
        jax.ShapeDtypeStruct((per_slab, 1, BLOCK), jnp.float32),
    ] + [
        jax.ShapeDtypeStruct((per_slab * half + mass_rows, BLOCK), jnp.bfloat16)
        for _ in range(slabs - 1)
    ]
    total = slabs * per_slab
    outs = pl.pallas_call(
        kernel,
        out_shape=out_shape,
        in_specs=[smem, smem] + [vmem] * (3 * slabs),
        out_specs=[vmem] * len(out_shape),
        scratch_shapes=[
            pltpu.VMEM((total, BLOCK, 2 * half), jnp.bfloat16),
            pltpu.VMEM((total, BLOCK, half), jnp.bfloat16),
            pltpu.VMEM((total, half, BLOCK), jnp.float32),
            pltpu.VMEM((total, 1, BLOCK), jnp.float32),
            pltpu.VMEM((2, BLOCK, K * BLOCK), jnp.float32),
            pltpu.VMEM((2, K * BLOCK, half), jnp.bfloat16),
            pltpu.SemaphoreType.DMA((3, slabs)),
        ],
    )(slot, active.reshape(-1), *window_e, *others, *window_v)
    own_num, own_mass = outs[0], outs[1]
    remote = outs[2:]
    offsets = [o for o in range(-hops, hops + 1) if o != 0]
    if not halo:
        arrivals = [passed_along(outgoing, "frame", offset) for offset, outgoing in zip(offsets, remote)]
        result = pl.pallas_call(
            functools.partial(combine_kernel, per_slab=per_slab, half=half),
            out_shape=jax.ShapeDtypeStruct((per_slab, BLOCK, half), jnp.bfloat16),
            in_specs=[vmem] * (3 + len(arrivals)),
            out_specs=vmem,
        )(own_num, own_mass, values.reshape(per_slab, BLOCK, half), *arrivals)
        return result.reshape(frames, band_rows, half)
    for offset, outgoing in zip(offsets, remote):
        arrived = passed_along(outgoing, "frame", offset).astype(jnp.float32)
        own_num = own_num + arrived[: per_slab * half].reshape(per_slab, half, BLOCK)
        own_mass = own_mass + arrived[per_slab * half : per_slab * half + per_slab][:, None, :]
    own_num = own_num.reshape(frames, rimmed_blocks, half, BLOCK)
    own_mass = own_mass.reshape(frames, rimmed_blocks, BLOCK)
    if halo:
        for toward in (1, -1):
            rim_block = blocks + 1 if toward > 0 else 0
            target_block = 1 if toward > 0 else blocks
            arrived = (
                passed_along(own_num[:, rim_block].astype(jnp.bfloat16), "band", toward).astype(
                    jnp.float32
                ),
                passed_along(own_mass[:, rim_block].astype(jnp.bfloat16), "band", toward).astype(
                    jnp.float32
                ),
            )
            own_num = own_num.at[:, target_block].add(arrived[0])
            own_mass = own_mass.at[:, target_block].add(arrived[1])
        own_num = own_num[:, 1 : blocks + 1]
        own_mass = own_mass[:, 1 : blocks + 1]
    numer = jnp.swapaxes(own_num, -1, -2)
    value_blocks = values.reshape(frames, blocks, BLOCK, half).astype(jnp.float32)
    result = (numer + value_blocks) / (own_mass[..., None] + 1.0)
    return result.reshape(frames, band_rows, half).astype(jnp.bfloat16)


def solution(mesh):
    placed = (
        P(("reel", "frame"), "band", "chan"),
        P(("reel", "frame"), "band", "chan"),
        P(("reel", "frame"), "band", None),
        P(("reel", "frame"), "band", None),
        P(("reel", "frame")),
    )
    return jax.shard_map(
        shards,
        mesh=mesh,
        in_specs=placed,
        out_specs=P(("reel", "frame"), "band", "chan"),
        check_vma=False,
    )
```

```python
import functools
import math

import jax
import jax.numpy as jnp
from jax import lax
from jax.experimental import pallas as pl
from jax.experimental.pallas import tpu as pltpu
from jax.sharding import PartitionSpec as P

W = 256
BLOCK = 128
K = 16
REACH = 8
MASS_ROWS = 16
GROUP = 4


def with_halo(x, sides, width):
    for axis, dim in sides:
        size, length = (lax.axis_size(axis), x.shape[dim])
        up = [(i, (i + 1) % size) for i in range(size - 1)]
        down = [(j, i) for i, j in up]
        last = lax.slice_in_dim(x, length - width, length, axis=dim)
        initial = lax.slice_in_dim(x, 0, width, axis=dim)
        before = lax.ppermute(last, axis, up)
        after = lax.ppermute(initial, axis, down)
        x = jnp.concatenate([before, x, after], axis=dim)
    return x


def passed_along(block, axis, distance):
    devices = range(lax.axis_size(axis))
    route = [(i - distance, i) for i in devices if i - distance in devices]
    return lax.ppermute(block, axis, route)


def aggregate_kernel(
    slot_ref, act_ref, *refs, slabs, per_slab, center, queries, half, blocks, rimmed, halo
):
    sources = [refs[:slabs], refs[2 * slabs : 3 * slabs], refs[slabs : 2 * slabs]]
    own_num_ref, own_mass_ref = refs[3 * slabs : 3 * slabs + 2]
    remote_refs = refs[3 * slabs + 2 : 4 * slabs + 1]
    key_e, key_v, acc, macc, score_ref, value_ref, sems = refs[4 * slabs + 1 :]

    copies = []
    for s in range(slabs):
        dst = pl.ds(s * per_slab, per_slab)
        targets = (
            key_e.at[dst, :, pl.ds(0, half)],
            key_v.at[dst],
            key_e.at[dst, :, pl.ds(half, half)],
        )
        for kind, target in enumerate(targets):
            copies.append(pltpu.make_async_copy(sources[kind][s], target, sems.at[kind, s]))
    for c in copies:
        c.start()
    acc[...] = jnp.zeros(acc.shape, acc.dtype)
    macc[...] = jnp.zeros(macc.shape, macc.dtype)
    for c in copies:
        c.wait()

    score_scale = 1.0 / math.sqrt(W)
    dims_t = (((1,), (1,)), ((), ()))

    def one_query(i, buf):
        q_slot = center + (i // blocks) * rimmed + halo + i % blocks
        query = key_e[q_slot] * jnp.asarray(score_scale, jnp.bfloat16)
        slots = [slot_ref[i * K + k] for k in range(K)]
        for k in range(K):
            s = slots[k]
            part = lax.dot_general(query, key_e[s], dims_t, preferred_element_type=jnp.float32)
            score_ref[buf, :, k * BLOCK : (k + 1) * BLOCK] = part
            value_ref[buf, k * BLOCK : (k + 1) * BLOCK, :] = key_v[s]
        score = score_ref[buf]
        peak = jnp.max(score, axis=-1, keepdims=True)
        exponent = jnp.exp(score - peak)
        prob = exponent / jnp.sum(exponent, axis=-1, keepdims=True)
        attention = prob.astype(jnp.bfloat16)
        estimate = jnp.dot(attention, value_ref[buf], preferred_element_type=jnp.float32)
        active = act_ref[i].astype(jnp.float32)
        estimate = estimate.astype(jnp.bfloat16).astype(jnp.float32) * active
        estimate_t = estimate.T.astype(jnp.bfloat16)
        contrib_t = jnp.dot(estimate_t, attention, preferred_element_type=jnp.float32)
        weights = jnp.sum(prob, axis=0, keepdims=True) * active
        for k in range(K):
            s = slots[k]
            acc[s] = acc[s] + contrib_t[:, k * BLOCK : (k + 1) * BLOCK]
            macc[s] = macc[s] + weights[:, k * BLOCK : (k + 1) * BLOCK]

    def query_group(p, carry):
        for b in range(GROUP):
            one_query(GROUP * p + b, b)
        return carry

    lax.fori_loop(0, queries // GROUP, query_group, 0)
    for b in range(queries % GROUP):
        one_query(queries - queries % GROUP + b, b)

    own = pl.ds(center, per_slab)
    own_num_ref[...] = acc[own]
    own_mass_ref[...] = macc[own]
    remote = [s for s in range(slabs) if s * per_slab != center]
    mass_rows = -(-per_slab // MASS_ROWS) * MASS_ROWS
    for ref, s in zip(remote_refs, remote):
        rows = pl.ds(s * per_slab, per_slab)
        ref[: per_slab * half, :] = acc[rows].reshape(per_slab * half, BLOCK).astype(jnp.bfloat16)
        spread = [macc[s * per_slab + j] for j in range(per_slab)]
        if mass_rows > per_slab:
            spread.append(jnp.zeros((mass_rows - per_slab, BLOCK), jnp.float32))
        ref[per_slab * half :, :] = jnp.concatenate(spread, axis=0).astype(jnp.bfloat16)


def combine_kernel(num_ref, mass_ref, values_ref, *refs, per_slab, half):
    arrived_refs = refs[:-1]
    out_ref = refs[-1]
    tail = per_slab * half
    masses = [ref[tail:, :].astype(jnp.float32) for ref in arrived_refs]
    for j in range(per_slab):
        numer = num_ref[j]
        mass = mass_ref[j]
        for ref, rows in zip(arrived_refs, masses):
            numer = numer + ref[j * half : (j + 1) * half, :].astype(jnp.float32)
            mass = mass + rows[j : j + 1]
        own = values_ref[j].astype(jnp.float32).T
        result = (numer + own) / (mass + 1.0)
        out_ref[j] = result.T.astype(jnp.bfloat16)


def shards(embed, values, match_frame, match_block, block_counts):
    frames = embed.shape[0]
    band_rows = embed.shape[1]
    half = embed.shape[2]
    blocks = band_rows // BLOCK
    hops = -(-REACH // frames)
    band_index = lax.axis_index("band")
    band_size = lax.axis_size("band")
    halo = 1 if band_size > 1 else 0
    chan_size = lax.axis_size("chan")
    chan_swap = [(i, (i + 1) % chan_size) for i in range(chan_size)]

    if halo:
        embed, rim_values = (with_halo(x, (("band", 1),), BLOCK) for x in (embed, values))
    else:
        rim_values = values
    rimmed_blocks = blocks + 2 * halo
    per_slab = frames * rimmed_blocks
    window_e = []
    window_v = []
    for offset in range(-hops, hops + 1):
        for own, window in ((embed, window_e), (rim_values, window_v)):
            slab = own if offset == 0 else passed_along(own, "frame", -offset)
            window.append(slab.reshape(per_slab, BLOCK, half))
    others = [lax.ppermute(slab, "chan", chan_swap) for slab in window_e]
    slabs = len(window_e)
    center = hops * per_slab

    frame_ids = jnp.arange(frames, dtype=jnp.int32)
    key_rows = (hops * frames + frame_ids[:, None, None] + match_frame) * rimmed_blocks
    key_cols = match_block - band_index * blocks + halo
    slot = jnp.clip(key_rows + key_cols, 0, slabs * per_slab - 1).astype(jnp.int32).reshape(-1)
    block_ids = band_index * blocks + jnp.arange(blocks, dtype=jnp.int32)
    active = (block_ids[None, :] < block_counts[:, None]).astype(jnp.int32)
    queries = frames * blocks

    kernel = functools.partial(
        aggregate_kernel,
        slabs=slabs,
        per_slab=per_slab,
        center=center,
        queries=queries,
        half=half,
        blocks=blocks,
        rimmed=rimmed_blocks,
        halo=halo,
    )
    smem = pl.BlockSpec(memory_space=pltpu.SMEM)
    hbm = pl.BlockSpec(memory_space=pl.ANY)
    vmem = pl.BlockSpec(memory_space=pltpu.VMEM)
    mass_rows = -(-per_slab // MASS_ROWS) * MASS_ROWS
    out_shape = [
        jax.ShapeDtypeStruct((per_slab, half, BLOCK), jnp.float32),
        jax.ShapeDtypeStruct((per_slab, 1, BLOCK), jnp.float32),
    ] + [
        jax.ShapeDtypeStruct((per_slab * half + mass_rows, BLOCK), jnp.bfloat16)
        for _ in range(slabs - 1)
    ]
    total = slabs * per_slab
    outs = pl.pallas_call(
        kernel,
        out_shape=out_shape,
        in_specs=[smem, smem] + [vmem] * (3 * slabs),
        out_specs=[vmem] * len(out_shape),
        scratch_shapes=[
            pltpu.VMEM((total, BLOCK, 2 * half), jnp.bfloat16),
            pltpu.VMEM((total, BLOCK, half), jnp.bfloat16),
            pltpu.VMEM((total, half, BLOCK), jnp.float32),
            pltpu.VMEM((total, 1, BLOCK), jnp.float32),
            pltpu.VMEM((GROUP, BLOCK, K * BLOCK), jnp.float32),
            pltpu.VMEM((GROUP, K * BLOCK, half), jnp.bfloat16),
            pltpu.SemaphoreType.DMA((3, slabs)),
        ],
    )(slot, active.reshape(-1), *window_e, *others, *window_v)
    own_num, own_mass = outs[0], outs[1]
    remote = outs[2:]
    offsets = [o for o in range(-hops, hops + 1) if o != 0]
    if not halo:
        arrivals = [passed_along(outgoing, "frame", offset) for offset, outgoing in zip(offsets, remote)]
        result = pl.pallas_call(
            functools.partial(combine_kernel, per_slab=per_slab, half=half),
            out_shape=jax.ShapeDtypeStruct((per_slab, BLOCK, half), jnp.bfloat16),
            in_specs=[vmem] * (3 + len(arrivals)),
            out_specs=vmem,
        )(own_num, own_mass, values.reshape(per_slab, BLOCK, half), *arrivals)
        return result.reshape(frames, band_rows, half)
    for offset, outgoing in zip(offsets, remote):
        arrived = passed_along(outgoing, "frame", offset).astype(jnp.float32)
        own_num = own_num + arrived[: per_slab * half].reshape(per_slab, half, BLOCK)
        own_mass = own_mass + arrived[per_slab * half : per_slab * half + per_slab][:, None, :]
    own_num = own_num.reshape(frames, rimmed_blocks, half, BLOCK)
    own_mass = own_mass.reshape(frames, rimmed_blocks, BLOCK)
    if halo:
        for toward in (1, -1):
            rim_block = blocks + 1 if toward > 0 else 0
            target_block = 1 if toward > 0 else blocks
            arrived = (
                passed_along(own_num[:, rim_block].astype(jnp.bfloat16), "band", toward).astype(
                    jnp.float32
                ),
                passed_along(own_mass[:, rim_block].astype(jnp.bfloat16), "band", toward).astype(
                    jnp.float32
                ),
            )
            own_num = own_num.at[:, target_block].add(arrived[0])
            own_mass = own_mass.at[:, target_block].add(arrived[1])
        own_num = own_num[:, 1 : blocks + 1]
        own_mass = own_mass[:, 1 : blocks + 1]
    numer = jnp.swapaxes(own_num, -1, -2)
    value_blocks = values.reshape(frames, blocks, BLOCK, half).astype(jnp.float32)
    result = (numer + value_blocks) / (own_mass[..., None] + 1.0)
    return result.reshape(frames, band_rows, half).astype(jnp.bfloat16)


def solution(mesh):
    placed = (
        P(("reel", "frame"), "band", "chan"),
        P(("reel", "frame"), "band", "chan"),
        P(("reel", "frame"), "band", None),
        P(("reel", "frame"), "band", None),
        P(("reel", "frame")),
    )
    return jax.shard_map(
        shards,
        mesh=mesh,
        in_specs=placed,
        out_specs=P(("reel", "frame"), "band", "chan"),
        check_vma=False,
    )
```

```python
import functools
import math

import jax
import jax.numpy as jnp
from jax import lax
from jax.experimental import pallas as pl
from jax.experimental.pallas import tpu as pltpu
from jax.sharding import PartitionSpec as P

W = 256
BLOCK = 128
K = 16
REACH = 8
MASS_ROWS = 16
GROUP = 4


def with_halo(x, sides, width):
    for axis, dim in sides:
        size, length = (lax.axis_size(axis), x.shape[dim])
        up = [(i, (i + 1) % size) for i in range(size - 1)]
        down = [(j, i) for i, j in up]
        last = lax.slice_in_dim(x, length - width, length, axis=dim)
        initial = lax.slice_in_dim(x, 0, width, axis=dim)
        before = lax.ppermute(last, axis, up)
        after = lax.ppermute(initial, axis, down)
        x = jnp.concatenate([before, x, after], axis=dim)
    return x


def passed_along(block, axis, distance):
    devices = range(lax.axis_size(axis))
    route = [(i - distance, i) for i in devices if i - distance in devices]
    return lax.ppermute(block, axis, route)


def aggregate_kernel(
    slot_ref, act_ref, *refs, slabs, per_slab, center, queries, half, blocks, rimmed, halo
):
    sources = [refs[:slabs], refs[2 * slabs : 3 * slabs], refs[slabs : 2 * slabs]]
    own_num_ref, own_mass_ref = refs[3 * slabs : 3 * slabs + 2]
    remote_refs = refs[3 * slabs + 2 : 4 * slabs + 1]
    key_e, key_v, acc, macc, score_ref, value_ref, sems = refs[4 * slabs + 1 :]

    copies = []
    for s in range(slabs):
        dst = pl.ds(s * per_slab, per_slab)
        targets = (
            key_e.at[dst, :, pl.ds(0, half)],
            key_v.at[dst],
            key_e.at[dst, :, pl.ds(half, half)],
        )
        for kind, target in enumerate(targets):
            copies.append(pltpu.make_async_copy(sources[kind][s], target, sems.at[kind, s]))
    for c in copies:
        c.start()
    acc[...] = jnp.zeros(acc.shape, acc.dtype)
    macc[...] = jnp.zeros(macc.shape, macc.dtype)
    if not halo:
        own_values = sources[1][center // per_slab]
        for j in range(per_slab):
            acc[center + j] = own_values[j].astype(jnp.float32).T
    for c in copies:
        c.wait()

    score_scale = 1.0 / math.sqrt(W)
    dims_t = (((1,), (1,)), ((), ()))

    def one_query(i, buf):
        q_slot = center + (i // blocks) * rimmed + halo + i % blocks
        query = key_e[q_slot] * jnp.asarray(score_scale, jnp.bfloat16)
        slots = [slot_ref[i * K + k] for k in range(K)]
        for k in range(K):
            s = slots[k]
            part = lax.dot_general(query, key_e[s], dims_t, preferred_element_type=jnp.float32)
            score_ref[buf, :, k * BLOCK : (k + 1) * BLOCK] = part
            value_ref[buf, k * BLOCK : (k + 1) * BLOCK, :] = key_v[s]
        score = score_ref[buf]
        peak = jnp.max(score, axis=-1, keepdims=True)
        exponent = jnp.exp(score - peak)
        prob = exponent / jnp.sum(exponent, axis=-1, keepdims=True)
        attention = prob.astype(jnp.bfloat16)
        estimate = jnp.dot(attention, value_ref[buf], preferred_element_type=jnp.float32)
        active = act_ref[i].astype(jnp.float32)
        estimate = estimate.astype(jnp.bfloat16).astype(jnp.float32) * active
        estimate_t = estimate.T.astype(jnp.bfloat16)
        contrib_t = jnp.dot(estimate_t, attention, preferred_element_type=jnp.float32)
        weights = jnp.sum(prob, axis=0, keepdims=True) * active
        for k in range(K):
            s = slots[k]
            acc[s] = acc[s] + contrib_t[:, k * BLOCK : (k + 1) * BLOCK]
            macc[s] = macc[s] + weights[:, k * BLOCK : (k + 1) * BLOCK]

    def query_group(p, carry):
        for b in range(GROUP):
            one_query(GROUP * p + b, b)
        return carry

    lax.fori_loop(0, queries // GROUP, query_group, 0)
    for b in range(queries % GROUP):
        one_query(queries - queries % GROUP + b, b)

    own = pl.ds(center, per_slab)
    own_num_ref[...] = acc[own]
    own_mass_ref[...] = macc[own]
    remote = [s for s in range(slabs) if s * per_slab != center]
    mass_rows = -(-per_slab // MASS_ROWS) * MASS_ROWS
    for ref, s in zip(remote_refs, remote):
        rows = pl.ds(s * per_slab, per_slab)
        ref[: per_slab * half, :] = acc[rows].reshape(per_slab * half, BLOCK).astype(jnp.bfloat16)
        spread = [macc[s * per_slab + j] for j in range(per_slab)]
        if mass_rows > per_slab:
            spread.append(jnp.zeros((mass_rows - per_slab, BLOCK), jnp.float32))
        ref[per_slab * half :, :] = jnp.concatenate(spread, axis=0).astype(jnp.bfloat16)


def combine_kernel(num_ref, mass_ref, *refs, per_slab, half):
    arrived_refs = refs[:-1]
    out_ref = refs[-1]
    tail = per_slab * half
    masses = [ref[tail:, :].astype(jnp.float32) for ref in arrived_refs]
    for j in range(per_slab):
        numer = num_ref[j]
        mass = mass_ref[j]
        for ref, rows in zip(arrived_refs, masses):
            numer = numer + ref[j * half : (j + 1) * half, :].astype(jnp.float32)
            mass = mass + rows[j : j + 1]
        result = numer / (mass + 1.0)
        out_ref[j] = result.T.astype(jnp.bfloat16)


def shards(embed, values, match_frame, match_block, block_counts):
    frames = embed.shape[0]
    band_rows = embed.shape[1]
    half = embed.shape[2]
    blocks = band_rows // BLOCK
    hops = -(-REACH // frames)
    band_index = lax.axis_index("band")
    band_size = lax.axis_size("band")
    halo = 1 if band_size > 1 else 0
    chan_size = lax.axis_size("chan")
    chan_swap = [(i, (i + 1) % chan_size) for i in range(chan_size)]

    if halo:
        embed, rim_values = (with_halo(x, (("band", 1),), BLOCK) for x in (embed, values))
    else:
        rim_values = values
    rimmed_blocks = blocks + 2 * halo
    per_slab = frames * rimmed_blocks
    window_e = []
    window_v = []
    for offset in range(-hops, hops + 1):
        for own, window in ((embed, window_e), (rim_values, window_v)):
            slab = own if offset == 0 else passed_along(own, "frame", -offset)
            window.append(slab.reshape(per_slab, BLOCK, half))
    others = [lax.ppermute(slab, "chan", chan_swap) for slab in window_e]
    slabs = len(window_e)
    center = hops * per_slab

    frame_ids = jnp.arange(frames, dtype=jnp.int32)
    key_rows = (hops * frames + frame_ids[:, None, None] + match_frame) * rimmed_blocks
    key_cols = match_block - band_index * blocks + halo
    slot = jnp.clip(key_rows + key_cols, 0, slabs * per_slab - 1).astype(jnp.int32).reshape(-1)
    block_ids = band_index * blocks + jnp.arange(blocks, dtype=jnp.int32)
    active = (block_ids[None, :] < block_counts[:, None]).astype(jnp.int32)
    queries = frames * blocks

    kernel = functools.partial(
        aggregate_kernel,
        slabs=slabs,
        per_slab=per_slab,
        center=center,
        queries=queries,
        half=half,
        blocks=blocks,
        rimmed=rimmed_blocks,
        halo=halo,
    )
    smem = pl.BlockSpec(memory_space=pltpu.SMEM)
    hbm = pl.BlockSpec(memory_space=pl.ANY)
    vmem = pl.BlockSpec(memory_space=pltpu.VMEM)
    mass_rows = -(-per_slab // MASS_ROWS) * MASS_ROWS
    out_shape = [
        jax.ShapeDtypeStruct((per_slab, half, BLOCK), jnp.float32),
        jax.ShapeDtypeStruct((per_slab, 1, BLOCK), jnp.float32),
    ] + [
        jax.ShapeDtypeStruct((per_slab * half + mass_rows, BLOCK), jnp.bfloat16)
        for _ in range(slabs - 1)
    ]
    total = slabs * per_slab
    outs = pl.pallas_call(
        kernel,
        out_shape=out_shape,
        in_specs=[smem, smem] + [vmem] * (3 * slabs),
        out_specs=[vmem] * len(out_shape),
        scratch_shapes=[
            pltpu.VMEM((total, BLOCK, 2 * half), jnp.bfloat16),
            pltpu.VMEM((total, BLOCK, half), jnp.bfloat16),
            pltpu.VMEM((total, half, BLOCK), jnp.float32),
            pltpu.VMEM((total, 1, BLOCK), jnp.float32),
            pltpu.VMEM((GROUP, BLOCK, K * BLOCK), jnp.float32),
            pltpu.VMEM((GROUP, K * BLOCK, half), jnp.bfloat16),
            pltpu.SemaphoreType.DMA((3, slabs)),
        ],
    )(slot, active.reshape(-1), *window_e, *others, *window_v)
    own_num, own_mass = outs[0], outs[1]
    remote = outs[2:]
    offsets = [o for o in range(-hops, hops + 1) if o != 0]
    if not halo:
        arrivals = [passed_along(outgoing, "frame", offset) for offset, outgoing in zip(offsets, remote)]
        result = pl.pallas_call(
            functools.partial(combine_kernel, per_slab=per_slab, half=half),
            out_shape=jax.ShapeDtypeStruct((per_slab, BLOCK, half), jnp.bfloat16),
            in_specs=[vmem] * (2 + len(arrivals)),
            out_specs=vmem,
        )(own_num, own_mass, *arrivals)
        return result.reshape(frames, band_rows, half)
    for offset, outgoing in zip(offsets, remote):
        arrived = passed_along(outgoing, "frame", offset).astype(jnp.float32)
        own_num = own_num + arrived[: per_slab * half].reshape(per_slab, half, BLOCK)
        own_mass = own_mass + arrived[per_slab * half : per_slab * half + per_slab][:, None, :]
    own_num = own_num.reshape(frames, rimmed_blocks, half, BLOCK)
    own_mass = own_mass.reshape(frames, rimmed_blocks, BLOCK)
    if halo:
        for toward in (1, -1):
            rim_block = blocks + 1 if toward > 0 else 0
            target_block = 1 if toward > 0 else blocks
            arrived = (
                passed_along(own_num[:, rim_block].astype(jnp.bfloat16), "band", toward).astype(
                    jnp.float32
                ),
                passed_along(own_mass[:, rim_block].astype(jnp.bfloat16), "band", toward).astype(
                    jnp.float32
                ),
            )
            own_num = own_num.at[:, target_block].add(arrived[0])
            own_mass = own_mass.at[:, target_block].add(arrived[1])
        own_num = own_num[:, 1 : blocks + 1]
        own_mass = own_mass[:, 1 : blocks + 1]
    numer = jnp.swapaxes(own_num, -1, -2)
    value_blocks = values.reshape(frames, blocks, BLOCK, half).astype(jnp.float32)
    result = (numer + value_blocks) / (own_mass[..., None] + 1.0)
    return result.reshape(frames, band_rows, half).astype(jnp.bfloat16)


def solution(mesh):
    placed = (
        P(("reel", "frame"), "band", "chan"),
        P(("reel", "frame"), "band", "chan"),
        P(("reel", "frame"), "band", None),
        P(("reel", "frame"), "band", None),
        P(("reel", "frame")),
    )
    return jax.shard_map(
        shards,
        mesh=mesh,
        in_specs=placed,
        out_specs=P(("reel", "frame"), "band", "chan"),
        check_vma=False,
    )
```
